512 devices in a mesh: dp: 8 (over z_lo), expert: 64 (over z_hi, y, x, core).
Axes of the slice: x: 4, y: 4, z: 16 (z_hi: 2, z_lo: 8; z = z_hi * 8 + z_lo), core: 2. Of those that a mesh axis runs over, the one named last changes fastest.
Arguments:
- tokens: bfloat16 [1024, 64, 2048], P('dp', 'expert'), may hold values from -6 to 6
- assignment: int32 [1024, 64], P('dp', 'expert'), may hold values from 0 to 63, as said below
- up_weight: bfloat16 [64, 2048, 4096], P('expert', None, 'dp'), may hold values from -0.125 to 0.125
- down_weight: bfloat16 [64, 4096, 2048], P('expert', 'dp'), may hold values from -0.09375 to 0.09375
- mode_bias: float32 [3, 2048], replicated, may hold values from -0.6 to 0.6
- projection: bfloat16 [2048, 768], P('dp'), may hold values from -0.125 to 0.125
- logit_scale: float32 [3], replicated, may hold values from 4 to 16
- modality: int32 [16, 64], P('dp', 'expert'), may hold values from 0 to 2
- pair_index: int32 [16, 64], P('dp', 'expert'), may hold values from 0 to 15, as said below
Outputs:
- loss: float32 [16, 64], P('dp', 'expert')
- emb_grad: float32 [16, 64, 768], P('dp', 'expert')
The draws below stay inside these ranges and needn't reach their ends.
Inputs may be any that keep to these rules, and one draw needn't show every extreme that they name: `assignment`: among the tokens of the devices of one dp index, every expert is named by exactly 128; one device names one expert at most 4 times, and every device names some expert exactly 4 times. The members of group x are the 16 samples (m, x); pair_index[m, x] names a member other than m.
All inputs are finite; a program needn't handle non-finite values.
Results may differ from the reference program's by a relative error of at most 0.015.
Values may be sent and summed in bfloat16 or wider, within the bound.
No kernel may reach another device: no remote copies, remote signals or barrier semaphores. Data moves between devices by JAX's collectives and lax.ppermute only.
A program may use at most 64 MiB of HBM per device.

```python
import math
import jax
import jax.numpy as jnp
from jax import lax

D = 2048
HID = 4096
EMB = 768
MODES = 3
PATCH = 64
TOK_DEV = 128
EXPERTS = 64
TOK_COL = 1024
GSIZE = 16
N_DP = 8


def draw_assignment(key, part):
    groups = TOK_COL // TOK_DEV
    mean_load = TOK_DEV // EXPERTS

    def one_group(group_key):
        spread_key, shift_key, source_key, target_key, order_key = jax.random.split(group_key, 5)
        load_shift = jax.random.randint(spread_key, (EXPERTS // 2,), -mean_load, mean_load + 1)
        load_shift = load_shift.at[0].set(mean_load)
        loads = jnp.stack([mean_load + load_shift, mean_load - load_shift], axis=1).reshape(EXPERTS)
        loads = loads[jax.random.permutation(shift_key, EXPERTS)]
        sources = jax.random.permutation(source_key, EXPERTS)
        targets = jax.random.permutation(target_key, EXPERTS)
        counts = loads[(targets[None, :] - sources[:, None]) % EXPERTS]
        bounds = jnp.cumsum(counts, axis=1)
        positions = jnp.arange(TOK_DEV)
        sorted_ids = jnp.sum((bounds[:, None, :] <= positions[None, :, None]).astype(jnp.int32), axis=2)
        device_keys = jax.random.split(order_key, EXPERTS)
        shuffled = jax.vmap(lambda device_key, id_row: id_row[jax.random.permutation(device_key, TOK_DEV)])(device_keys, sorted_ids)
        return shuffled.T
    blocks = jax.vmap(one_group)(jax.random.split(key, groups))
    return blocks.reshape(TOK_COL, EXPERTS).astype(jnp.int32)


def draw_pair_index(key, part):
    offsets = jax.random.randint(key, (GSIZE, EXPERTS), 1, GSIZE)
    member = jnp.arange(GSIZE)[:, None]
    return ((member + offsets) % GSIZE).astype(jnp.int32)


def place_ends(array, own_key, low, high):
    longest = array.shape.index(max(array.shape))
    spots = []
    for shift in (0, 1):
        where = [jax.random.randint(jax.random.fold_in(own_key, axis), (), 0, length) for axis, length in enumerate(array.shape)]
        where[longest] = (where[longest] + shift) % array.shape[longest]
        spots.append(tuple(where))
    return array.at[spots[0]].set(low).at[spots[1]].set(high)


def level_of(own_key, extent, shards, smallest, largest):
    loudness, own = 1.0, jax.random.fold_in(own_key, 6)
    for position, blocks in shards:
        steps = jnp.exp(jax.random.uniform(jax.random.fold_in(own, position), (blocks,), jnp.float32, smallest / len(shards), largest / len(shards)))
        loudness = loudness * jnp.repeat(steps, extent[position] // blocks).reshape([-1 if axis == position else 1 for axis in range(len(extent))])
    return loudness


def centred(key, dims, width, limit, cuts=(), kind=jnp.bfloat16):
    factor_of = level_of(key, dims, cuts, -0.22, 0.18) if cuts else 1.0
    entries = jax.random.normal(key, dims, jnp.float32) * width * factor_of
    return jnp.minimum(jnp.maximum(entries, -limit), limit).astype(kind)


def setup_inputs(seed: int = 0) -> dict:
    key_of = jax.random.split(jax.random.key(seed), 10)
    return {
        "tokens": centred(key_of[0], (TOK_COL, EXPERTS, D), 1.0, 6.0, ((0, 8), (1, 64))),
        "assignment": draw_assignment(jax.random.fold_in(key_of[9], 71), 0),
        "up_weight": centred(key_of[2], (EXPERTS, D, HID), D ** -0.5, 0.125, ((0, 64), (2, 8))),
        "down_weight": centred(key_of[3], (EXPERTS, HID, D), HID ** -0.5, 0.09375, ((0, 64), (1, 8))),
        "mode_bias": centred(key_of[4], (MODES, D), 0.1, 0.6, (), jnp.float32),
        "projection": centred(key_of[5], (D, EMB), D ** -0.5, 0.125, ((0, 8),)),
        "logit_scale": jnp.clip(jnp.exp(jax.random.uniform(key_of[6], (MODES,), jnp.float32, math.log(4.0), math.log(16.0))), 4.0, 16.0),
        "modality": place_ends(jax.random.randint(key_of[7], (GSIZE, EXPERTS), 0, MODES), jax.random.fold_in(key_of[7], 1), 0, MODES - 1).astype(jnp.int32),
        "pair_index": draw_pair_index(jax.random.fold_in(key_of[9], 71), 0),
    }


def group_losses(raw_rows, anchor_scale, target_index):
    member_count = raw_rows.shape[0]
    norm_square = lax.optimization_barrier(jnp.sum(raw_rows * raw_rows, axis=-1, keepdims=True))
    unit_rows = raw_rows / jnp.sqrt(norm_square + 1e-06)
    scores = anchor_scale[:, None] * jnp.dot(unit_rows, unit_rows.T, precision=lax.Precision.HIGHEST)
    member = jnp.arange(member_count, dtype=jnp.int32)
    is_self = member[:, None] == member[None, :]
    denominator = lax.optimization_barrier(jnp.sum(jnp.where(is_self, 0.0, jnp.exp(scores)), axis=-1))
    positive = lax.optimization_barrier(jnp.sum(jnp.where(member[None, :] == target_index[:, None], scores, 0.0), axis=-1))
    return jnp.log(denominator) - positive

def losses_and_grads(raw_rows, anchor_scale, target_index):
    losses, pullback = jax.vjp(lambda rows_in: group_losses(rows_in, anchor_scale, target_index), raw_rows)
    row_grads, = pullback(jnp.ones_like(losses))
    return (losses, row_grads)

def reference(tokens, assignment, up_weight, down_weight, mode_bias, projection, logit_scale, modality, pair_index):
    flat_tokens = tokens.reshape(TOK_COL * EXPERTS, D)
    flat_assign = assignment.reshape(-1)
    order_rows = jnp.argsort(flat_assign, stable=True).astype(jnp.int32).reshape(EXPERTS, TOK_COL)
    slice_width = HID // N_DP

    def run_expert(pooled_sum, packed):
        row_ids, up_mat, down_mat = packed
        rows_in = flat_tokens[row_ids].astype(jnp.float32)
        hidden = jax.nn.gelu(jnp.dot(rows_in, up_mat.astype(jnp.float32), preferred_element_type=jnp.float32, precision=lax.Precision.HIGHEST), approximate=False).astype(jnp.bfloat16)
        hidden_parts = hidden.astype(jnp.float32).reshape(TOK_COL, N_DP, slice_width)
        down_parts = down_mat.astype(jnp.float32).reshape(N_DP, slice_width, D)
        partial_value = jnp.einsum('rnh,nhd->nrd', hidden_parts, down_parts, precision=lax.Precision.HIGHEST)
        rounded = lax.optimization_barrier(partial_value.astype(jnp.bfloat16)).astype(jnp.float32)
        expert_out = lax.optimization_barrier(jnp.sum(rounded, axis=0))
        token_row = row_ids // EXPERTS
        token_col = row_ids % EXPERTS
        sample_ids = token_row // PATCH * EXPERTS + token_col
        return (pooled_sum.at[sample_ids].add(expert_out), None)
    start_sum = jnp.zeros((GSIZE * EXPERTS, D), jnp.float32)
    ffn_sum, _ = lax.scan(run_expert, start_sum, (order_rows, up_weight, down_weight))
    token_sum = lax.optimization_barrier(jnp.sum(tokens.reshape(GSIZE, PATCH, EXPERTS, D), axis=1, dtype=jnp.float32))
    pooled = (token_sum + ffn_sum.reshape(GSIZE, EXPERTS, D)) / PATCH
    feature = (pooled + mode_bias[modality]).astype(jnp.bfloat16)
    embedding = jnp.einsum('gxd,de->gxe', feature.astype(jnp.float32), projection.astype(jnp.float32), precision=lax.Precision.HIGHEST)
    anchor_scale = logit_scale[modality]
    loss, emb_grad = jax.vmap(losses_and_grads, in_axes=(1, 1, 1), out_axes=(1, 1))(embedding, anchor_scale, pair_index)
    return (loss, emb_grad)
```

```python
import jax
import jax.numpy as jnp
from jax import lax
from jax.sharding import PartitionSpec as P

PATCH = 64
EMPTY = 64.0


def group_losses(raw_rows, anchor_scale, target_index):
    member_count = raw_rows.shape[0]
    norm_square = jnp.sum(raw_rows * raw_rows, axis=-1, keepdims=True)
    unit_rows = raw_rows / jnp.sqrt(norm_square + 1e-06)
    scores = anchor_scale[:, None] * jnp.dot(
        unit_rows, unit_rows.T, precision=lax.Precision.HIGHEST
    )
    member = jnp.arange(member_count, dtype=jnp.int32)
    is_self = member[:, None] == member[None, :]
    denominator = jnp.sum(jnp.where(is_self, 0.0, jnp.exp(scores)), axis=-1)
    positive = jnp.sum(jnp.where(member[None, :] == target_index[:, None], scores, 0.0), axis=-1)
    return jnp.log(denominator) - positive


def losses_and_grads(raw_rows, anchor_scale, target_index):
    losses, pullback = jax.vjp(
        lambda rows_in: group_losses(rows_in, anchor_scale, target_index), raw_rows
    )
    (row_grads,) = pullback(jnp.ones_like(losses))
    return (losses, row_grads)


def shards(
    tokens,
    assignment,
    up_weight,
    down_weight,
    mode_bias,
    projection,
    logit_scale,
    modality,
    pair_index,
):
    tok_rows = tokens.shape[0]
    model_width = tokens.shape[2]
    experts = lax.axis_size("expert")
    n_dp = lax.axis_size("dp")
    capacity = 2 * tok_rows // experts
    samples_dev = tok_rows // PATCH
    dp_index = lax.axis_index("dp")
    own_tokens = tokens[:, 0, :]
    own_assign = assignment[:, 0]
    expert_ids = jnp.arange(experts, dtype=jnp.int32)
    one_hot = (own_assign[:, None] == expert_ids[None, :]).astype(jnp.int32)
    running = jnp.cumsum(one_hot, axis=0)
    rank_in = jnp.sum(one_hot * (running - 1), axis=1)
    slot_ids = own_assign * capacity + rank_in
    empty_rows = jnp.zeros((experts * capacity, model_width), jnp.bfloat16).at[:, 0].set(EMPTY)
    send_rows = empty_rows.at[slot_ids].set(own_tokens)
    send_rows = send_rows.reshape(experts, capacity, model_width)
    recv_rows = lax.all_to_all(send_rows, "expert", split_axis=0, concat_axis=0, tiled=True)
    is_valid = recv_rows[:, :, 0] < EMPTY * 0.5
    src_totals = jnp.sum(is_valid.astype(jnp.int32), axis=1)
    offsets = jnp.cumsum(src_totals) - src_totals
    slot_pos = jnp.arange(capacity, dtype=jnp.int32)
    dest_rows = jnp.where(is_valid, offsets[:, None] + slot_pos[None, :], tok_rows)
    compact = (
        jnp.zeros((tok_rows, model_width), jnp.bfloat16)
        .at[dest_rows.reshape(-1)]
        .set(recv_rows.reshape(-1, model_width), mode="drop")
    )
    up_local = up_weight[0]
    down_local = down_weight[0]
    hidden = jax.nn.gelu(
        jnp.dot(
            lax.all_gather(compact, "dp", axis=0, tiled=True),
            up_local,
            preferred_element_type=jnp.float32,
        ),
        approximate=False,
    ).astype(jnp.bfloat16)
    expert_out = lax.psum_scatter(
        jnp.dot(hidden, down_local, preferred_element_type=jnp.float32).astype(jnp.bfloat16),
        "dp",
        scatter_dimension=0,
        tiled=True,
    ).astype(jnp.float32)
    slot_out = (
        jnp.take(expert_out, jnp.minimum(dest_rows, tok_rows - 1), axis=0) * is_valid[:, :, None]
    )
    returned = lax.all_to_all(
        slot_out.astype(jnp.bfloat16), "expert", split_axis=0, concat_axis=0, tiled=True
    ).astype(slot_out.dtype)
    token_out = jnp.take(returned.reshape(experts * capacity, model_width), slot_ids, axis=0)
    ffn_pool = jnp.sum(token_out.reshape(samples_dev, PATCH, model_width), axis=1)
    token_sum = jnp.sum(
        own_tokens.reshape(samples_dev, PATCH, model_width), axis=1, dtype=jnp.float32
    )
    pooled = (token_sum + ffn_pool) / PATCH
    own_mode = modality[:, 0]
    mode_ids = jnp.arange(mode_bias.shape[0], dtype=jnp.int32)
    mode_match = own_mode[:, None] == mode_ids[None, :]
    bias_rows = jnp.sum(jnp.where(mode_match[:, :, None], mode_bias[None, :, :], 0.0), axis=1)
    feature = (pooled + bias_rows).astype(jnp.bfloat16)
    block = model_width // n_dp
    meta_width = 128
    meta = jnp.concatenate(
        [
            jnp.broadcast_to(own_mode[:, None], (samples_dev, meta_width // 2)),
            jnp.broadcast_to(pair_index[:, 0][:, None], (samples_dev, meta_width // 2)),
        ],
        axis=1,
    ).astype(jnp.bfloat16)
    feat_blocks = feature.reshape(samples_dev, n_dp, block).transpose(1, 0, 2)
    packed = jnp.concatenate(
        [feat_blocks, jnp.broadcast_to(meta[None], (n_dp, samples_dev, meta_width))], axis=2
    )
    got = lax.all_to_all(packed, "dp", split_axis=0, concat_axis=0, tiled=True)
    got = got.reshape(n_dp * samples_dev, block + meta_width)
    all_feat = got[:, :block]
    all_mode = got[:, block].astype(jnp.int32)
    all_target = got[:, block + meta_width // 2].astype(jnp.int32)
    part_embed = jnp.dot(all_feat, projection, preferred_element_type=jnp.float32)
    all_embed = lax.psum(part_embed, "dp")
    all_match = all_mode[:, None] == mode_ids[None, :]
    all_scale = jnp.sum(jnp.where(all_match, logit_scale[None, :], 0.0), axis=1)
    losses, emb_grads = losses_and_grads(all_embed, all_scale, all_target)
    row_start = dp_index * samples_dev
    own_loss = lax.dynamic_slice_in_dim(losses, row_start, samples_dev, 0)
    own_grad = lax.dynamic_slice_in_dim(emb_grads, row_start, samples_dev, 0)
    return (own_loss[:, None], own_grad[:, None, :])


def solution(mesh):
    placed = (
        P("dp", "expert", None),
        P("dp", "expert"),
        P("expert", None, "dp"),
        P("expert", "dp", None),
        P(),
        P("dp", None),
        P(),
        P("dp", "expert"),
        P("dp", "expert"),
    )
    return jax.shard_map(
        shards,
        mesh=mesh,
        in_specs=placed,
        out_specs=(P("dp", "expert"), P("dp", "expert", None)),
        check_vma=False,
    )
```

```python
import jax
import jax.numpy as jnp
from jax import lax
from jax.sharding import PartitionSpec as P

PATCH = 64
EMPTY = 64.0


def group_losses(raw_rows, anchor_scale, target_index):
    member_count = raw_rows.shape[0]
    norm_square = jnp.sum(raw_rows * raw_rows, axis=-1, keepdims=True)
    unit_rows = raw_rows / jnp.sqrt(norm_square + 1e-06)
    scores = anchor_scale[:, None] * jnp.dot(
        unit_rows, unit_rows.T, precision=lax.Precision.HIGHEST
    )
    member = jnp.arange(member_count, dtype=jnp.int32)
    is_self = member[:, None] == member[None, :]
    denominator = jnp.sum(jnp.where(is_self, 0.0, jnp.exp(scores)), axis=-1)
    positive = jnp.sum(jnp.where(member[None, :] == target_index[:, None], scores, 0.0), axis=-1)
    return jnp.log(denominator) - positive


def losses_and_grads(raw_rows, anchor_scale, target_index):
    losses, pullback = jax.vjp(
        lambda rows_in: group_losses(rows_in, anchor_scale, target_index), raw_rows
    )
    (row_grads,) = pullback(jnp.ones_like(losses))
    return (losses, row_grads)


def shards(
    tokens,
    assignment,
    up_weight,
    down_weight,
    mode_bias,
    projection,
    logit_scale,
    modality,
    pair_index,
):
    tok_rows = tokens.shape[0]
    model_width = tokens.shape[2]
    experts = lax.axis_size("expert")
    n_dp = lax.axis_size("dp")
    capacity = 2 * tok_rows // experts
    samples_dev = tok_rows // PATCH
    dp_index = lax.axis_index("dp")
    own_tokens = tokens[:, 0, :]
    own_assign = assignment[:, 0]
    expert_ids = jnp.arange(experts, dtype=jnp.int32)
    one_hot = (own_assign[:, None] == expert_ids[None, :]).astype(jnp.int32)
    running = jnp.cumsum(one_hot, axis=0)
    rank_in = jnp.sum(one_hot * (running - 1), axis=1)
    slot_ids = own_assign * capacity + rank_in
    empty_rows = jnp.zeros((experts * capacity, model_width), jnp.bfloat16).at[:, 0].set(EMPTY)
    send_rows = empty_rows.at[slot_ids].set(own_tokens)
    send_rows = send_rows.reshape(experts, capacity, model_width)
    recv_rows = lax.all_to_all(send_rows, "expert", split_axis=0, concat_axis=0, tiled=True)
    is_valid = recv_rows[:, :, 0] < EMPTY * 0.5
    src_totals = jnp.sum(is_valid.astype(jnp.int32), axis=1)
    offsets = jnp.cumsum(src_totals) - src_totals
    slot_pos = jnp.arange(capacity, dtype=jnp.int32)
    dest_rows = jnp.where(is_valid, offsets[:, None] + slot_pos[None, :], tok_rows)
    compact = (
        jnp.zeros((tok_rows, model_width), jnp.bfloat16)
        .at[dest_rows.reshape(-1)]
        .set(recv_rows.reshape(-1, model_width), mode="drop")
    )
    up_local = up_weight[0]
    down_local = down_weight[0]
    head = lax.all_gather(projection, "dp", axis=0, tiled=True)
    fold = jnp.dot(down_local, head, preferred_element_type=jnp.float32)
    fold_hi = fold.astype(jnp.bfloat16)
    fold_lo = (fold - fold_hi.astype(jnp.float32)).astype(jnp.bfloat16)
    hidden = jax.nn.gelu(
        jnp.dot(
            lax.all_gather(compact, "dp", axis=0, tiled=True),
            up_local,
            preferred_element_type=jnp.float32,
        ),
        approximate=False,
    ).astype(jnp.bfloat16)
    part_embed = jnp.dot(hidden, fold_hi, preferred_element_type=jnp.float32) + jnp.dot(
        hidden, fold_lo, preferred_element_type=jnp.float32
    )
    expert_out = lax.psum_scatter(
        part_embed.astype(jnp.bfloat16), "dp", scatter_dimension=0, tiled=True
    ).astype(jnp.float32)
    emb_width = expert_out.shape[1]
    slot_out = (
        jnp.take(expert_out, jnp.minimum(dest_rows, tok_rows - 1), axis=0) * is_valid[:, :, None]
    )
    returned = lax.all_to_all(
        slot_out.astype(jnp.bfloat16), "expert", split_axis=0, concat_axis=0, tiled=True
    ).astype(slot_out.dtype)
    token_out = jnp.take(returned.reshape(experts * capacity, emb_width), slot_ids, axis=0)
    ffn_pool = jnp.sum(token_out.reshape(samples_dev, PATCH, emb_width), axis=1)
    token_sum = jnp.sum(
        own_tokens.reshape(samples_dev, PATCH, model_width), axis=1, dtype=jnp.float32
    )
    own_mode = modality[:, 0]
    mode_ids = jnp.arange(mode_bias.shape[0], dtype=jnp.int32)
    mode_match = own_mode[:, None] == mode_ids[None, :]
    bias_rows = jnp.sum(jnp.where(mode_match[:, :, None], mode_bias[None, :, :], 0.0), axis=1)
    base = token_sum / PATCH + bias_rows
    own_embed = ffn_pool / PATCH + jnp.dot(
        base, head.astype(jnp.float32), precision=lax.Precision.HIGHEST
    )
    own_scale = jnp.sum(jnp.where(mode_match, logit_scale[None, :], 0.0), axis=1)
    own_target = pair_index[:, 0].astype(jnp.float32)
    meta_width = 128
    meta = jnp.concatenate(
        [
            jnp.broadcast_to(own_scale[:, None], (samples_dev, meta_width // 2)),
            jnp.broadcast_to(own_target[:, None], (samples_dev, meta_width // 2)),
        ],
        axis=1,
    )
    got = lax.all_gather(
        jnp.concatenate([own_embed, meta], axis=1), "dp", axis=0, tiled=True
    )
    all_embed = got[:, :emb_width]
    all_scale = got[:, emb_width]
    all_target = got[:, emb_width + meta_width // 2].astype(jnp.int32)
    losses, emb_grads = losses_and_grads(all_embed, all_scale, all_target)
    row_start = dp_index * samples_dev
    own_loss = lax.dynamic_slice_in_dim(losses, row_start, samples_dev, 0)
    own_grad = lax.dynamic_slice_in_dim(emb_grads, row_start, samples_dev, 0)
    return (own_loss[:, None], own_grad[:, None, :])


def solution(mesh):
    placed = (
        P("dp", "expert", None),
        P("dp", "expert"),
        P("expert", None, "dp"),
        P("expert", "dp", None),
        P(),
        P("dp", None),
        P(),
        P("dp", "expert"),
        P("dp", "expert"),
    )
    return jax.shard_map(
        shards,
        mesh=mesh,
        in_specs=placed,
        out_specs=(P("dp", "expert"), P("dp", "expert", None)),
        check_vma=False,
    )
```

```python
import jax
import jax.numpy as jnp
from jax import lax
from jax.sharding import PartitionSpec as P

PATCH = 64
EMPTY = 64.0


def group_losses(raw_rows, anchor_scale, target_index):
    member_count = raw_rows.shape[0]
    norm_square = jnp.sum(raw_rows * raw_rows, axis=-1, keepdims=True)
    unit_rows = raw_rows / jnp.sqrt(norm_square + 1e-06)
    scores = anchor_scale[:, None] * jnp.dot(
        unit_rows, unit_rows.T, precision=lax.Precision.HIGHEST
    )
    member = jnp.arange(member_count, dtype=jnp.int32)
    is_self = member[:, None] == member[None, :]
    denominator = jnp.sum(jnp.where(is_self, 0.0, jnp.exp(scores)), axis=-1)
    positive = jnp.sum(jnp.where(member[None, :] == target_index[:, None], scores, 0.0), axis=-1)
    return jnp.log(denominator) - positive


def losses_and_grads(raw_rows, anchor_scale, target_index):
    losses, pullback = jax.vjp(
        lambda rows_in: group_losses(rows_in, anchor_scale, target_index), raw_rows
    )
    (row_grads,) = pullback(jnp.ones_like(losses))
    return (losses, row_grads)


def shards(
    tokens,
    assignment,
    up_weight,
    down_weight,
    mode_bias,
    projection,
    logit_scale,
    modality,
    pair_index,
):
    tok_rows = tokens.shape[0]
    model_width = tokens.shape[2]
    experts = lax.axis_size("expert")
    n_dp = lax.axis_size("dp")
    capacity = 2 * tok_rows // experts
    samples_dev = tok_rows // PATCH
    dp_index = lax.axis_index("dp")
    own_tokens = tokens[:, 0, :]
    own_assign = assignment[:, 0]
    expert_ids = jnp.arange(experts, dtype=jnp.int32)
    one_hot = (own_assign[:, None] == expert_ids[None, :]).astype(jnp.int32)
    running = jnp.cumsum(one_hot, axis=0)
    rank_in = jnp.sum(one_hot * (running - 1), axis=1)
    slot_ids = own_assign * capacity + rank_in
    empty_rows = jnp.zeros((experts * capacity, model_width), jnp.bfloat16).at[:, 0].set(EMPTY)
    send_rows = empty_rows.at[slot_ids].set(own_tokens)
    send_rows = send_rows.reshape(experts, capacity, model_width)
    recv_rows = lax.all_to_all(send_rows, "expert", split_axis=0, concat_axis=0, tiled=True)
    is_valid = recv_rows[:, :, 0] < EMPTY * 0.5
    src_totals = jnp.sum(is_valid.astype(jnp.int32), axis=1)
    offsets = jnp.cumsum(src_totals) - src_totals
    slot_pos = jnp.arange(capacity, dtype=jnp.int32)
    dest_rows = jnp.where(is_valid, offsets[:, None] + slot_pos[None, :], tok_rows)
    compact = (
        jnp.zeros((tok_rows, model_width), jnp.bfloat16)
        .at[dest_rows.reshape(-1)]
        .set(recv_rows.reshape(-1, model_width), mode="drop")
    )
    up_local = up_weight[0]
    down_local = down_weight[0]
    core = lax.axis_index("expert") % 2
    half = projection.shape[1] // 2
    own_cols = lax.dynamic_slice_in_dim(projection, core * half, half, 1)
    own_half = lax.all_gather(own_cols, "dp", axis=0, tiled=True)
    other_half = lax.ppermute(own_half, "expert", [(e, e ^ 1) for e in range(experts)])
    head = jnp.where(
        core == 0,
        jnp.concatenate([own_half, other_half], axis=1),
        jnp.concatenate([other_half, own_half], axis=1),
    )
    fold = jnp.dot(down_local, head, preferred_element_type=jnp.float32)
    fold_hi = fold.astype(jnp.bfloat16)
    fold_lo = (fold - fold_hi.astype(jnp.float32)).astype(jnp.bfloat16)
    hidden = jax.nn.gelu(
        jnp.dot(
            lax.all_gather(compact, "dp", axis=0, tiled=True),
            up_local,
            preferred_element_type=jnp.float32,
        ),
        approximate=False,
    ).astype(jnp.bfloat16)
    part_embed = jnp.dot(hidden, fold_hi, preferred_element_type=jnp.float32) + jnp.dot(
        hidden, fold_lo, preferred_element_type=jnp.float32
    )
    expert_out = lax.psum_scatter(
        part_embed.astype(jnp.bfloat16), "dp", scatter_dimension=0, tiled=True
    ).astype(jnp.float32)
    emb_width = expert_out.shape[1]
    slot_out = (
        jnp.take(expert_out, jnp.minimum(dest_rows, tok_rows - 1), axis=0) * is_valid[:, :, None]
    )
    returned = lax.all_to_all(
        slot_out.astype(jnp.bfloat16), "expert", split_axis=0, concat_axis=0, tiled=True
    ).astype(slot_out.dtype)
    token_out = jnp.take(returned.reshape(experts * capacity, emb_width), slot_ids, axis=0)
    ffn_pool = jnp.sum(token_out.reshape(samples_dev, PATCH, emb_width), axis=1)
    token_sum = jnp.sum(
        own_tokens.reshape(samples_dev, PATCH, model_width), axis=1, dtype=jnp.float32
    )
    own_mode = modality[:, 0]
    mode_ids = jnp.arange(mode_bias.shape[0], dtype=jnp.int32)
    mode_match = own_mode[:, None] == mode_ids[None, :]
    bias_rows = jnp.sum(jnp.where(mode_match[:, :, None], mode_bias[None, :, :], 0.0), axis=1)
    base = token_sum / PATCH + bias_rows
    own_embed = ffn_pool / PATCH + jnp.dot(
        base, head.astype(jnp.float32), precision=lax.Precision.HIGHEST
    )
    own_scale = jnp.sum(jnp.where(mode_match, logit_scale[None, :], 0.0), axis=1)
    own_target = pair_index[:, 0].astype(jnp.float32)
    meta_width = 128
    meta = jnp.concatenate(
        [
            jnp.broadcast_to(own_scale[:, None], (samples_dev, meta_width // 2)),
            jnp.broadcast_to(own_target[:, None], (samples_dev, meta_width // 2)),
        ],
        axis=1,
    )
    rows = jnp.concatenate([own_embed, meta], axis=1)
    got = lax.all_to_all(
        jnp.broadcast_to(rows[None], (n_dp,) + rows.shape), "dp", 0, 0, tiled=True
    ).reshape(n_dp * samples_dev, rows.shape[1])
    all_embed = got[:, :emb_width]
    all_scale = got[:, emb_width]
    all_target = got[:, emb_width + meta_width // 2].astype(jnp.int32)
    losses, emb_grads = losses_and_grads(all_embed, all_scale, all_target)
    row_start = dp_index * samples_dev
    own_loss = lax.dynamic_slice_in_dim(losses, row_start, samples_dev, 0)
    own_grad = lax.dynamic_slice_in_dim(emb_grads, row_start, samples_dev, 0)
    return (own_loss[:, None], own_grad[:, None, :])


def solution(mesh):
    placed = (
        P("dp", "expert", None),
        P("dp", "expert"),
        P("expert", None, "dp"),
        P("expert", "dp", None),
        P(),
        P("dp", None),
        P(),
        P("dp", "expert"),
        P("dp", "expert"),
    )
    return jax.shard_map(
        shards,
        mesh=mesh,
        in_specs=placed,
        out_specs=(P("dp", "expert"), P("dp", "expert", None)),
        check_vma=False,
    )
```

```python
import jax
import jax.numpy as jnp
from jax import lax
from jax.sharding import PartitionSpec as P

PATCH = 64
EMPTY = 64.0


def group_losses(raw_rows, anchor_scale, target_index):
    member_count = raw_rows.shape[0]
    norm_square = jnp.sum(raw_rows * raw_rows, axis=-1, keepdims=True)
    unit_rows = raw_rows / jnp.sqrt(norm_square + 1e-06)
    scores = anchor_scale[:, None] * jnp.dot(
        unit_rows, unit_rows.T, precision=lax.Precision.HIGHEST
    )
    member = jnp.arange(member_count, dtype=jnp.int32)
    is_self = member[:, None] == member[None, :]
    denominator = jnp.sum(jnp.where(is_self, 0.0, jnp.exp(scores)), axis=-1)
    positive = jnp.sum(jnp.where(member[None, :] == target_index[:, None], scores, 0.0), axis=-1)
    return jnp.log(denominator) - positive


def losses_and_grads(raw_rows, anchor_scale, target_index):
    losses, pullback = jax.vjp(
        lambda rows_in: group_losses(rows_in, anchor_scale, target_index), raw_rows
    )
    (row_grads,) = pullback(jnp.ones_like(losses))
    return (losses, row_grads)


def ring_gather(piece, dp_index, n_dp, experts):
    flip = experts // 2
    size = n_dp * experts
    up = []
    for d in range(n_dp):
        for e in range(experts):
            to = (d + 1, e) if d + 1 < n_dp else (0, e ^ flip)
            up.append((d * experts + e, to[0] * experts + to[1]))
    down = [(b, a) for a, b in up]
    assert len(set(b for _, b in up)) == size
    rows = piece.shape[0]
    out = jnp.zeros((n_dp, rows) + piece.shape[1:], piece.dtype)
    out = lax.dynamic_update_index_in_dim(out, piece, dp_index, 0)
    from_below = piece
    from_above = piece
    reach = n_dp // 2
    for step in range(1, reach):
        from_below = lax.ppermute(from_below, ("dp", "expert"), up)
        from_above = lax.ppermute(from_above, ("dp", "expert"), down)
        out = lax.dynamic_update_index_in_dim(out, from_below, (dp_index - step) % n_dp, 0)
        out = lax.dynamic_update_index_in_dim(out, from_above, (dp_index + step) % n_dp, 0)
    last_below = lax.ppermute(from_below[: rows // 2], ("dp", "expert"), up)
    last_above = lax.ppermute(from_above[rows // 2 :], ("dp", "expert"), down)
    last = jnp.concatenate([last_below, last_above], axis=0)
    out = lax.dynamic_update_index_in_dim(out, last, (dp_index + reach) % n_dp, 0)
    return out.reshape((n_dp * rows,) + piece.shape[1:])


def shards(
    tokens,
    assignment,
    up_weight,
    down_weight,
    mode_bias,
    projection,
    logit_scale,
    modality,
    pair_index,
):
    tok_rows = tokens.shape[0]
    model_width = tokens.shape[2]
    experts = lax.axis_size("expert")
    n_dp = lax.axis_size("dp")
    capacity = 2 * tok_rows // experts
    samples_dev = tok_rows // PATCH
    dp_index = lax.axis_index("dp")
    own_tokens = tokens[:, 0, :]
    own_assign = assignment[:, 0]
    expert_ids = jnp.arange(experts, dtype=jnp.int32)
    one_hot = (own_assign[:, None] == expert_ids[None, :]).astype(jnp.int32)
    running = jnp.cumsum(one_hot, axis=0)
    rank_in = jnp.sum(one_hot * (running - 1), axis=1)
    slot_ids = own_assign * capacity + rank_in
    empty_rows = jnp.zeros((experts * capacity, model_width), jnp.bfloat16).at[:, 0].set(EMPTY)
    send_rows = empty_rows.at[slot_ids].set(own_tokens)
    send_rows = send_rows.reshape(experts, capacity, model_width)
    recv_rows = lax.all_to_all(send_rows, "expert", split_axis=0, concat_axis=0, tiled=True)
    is_valid = recv_rows[:, :, 0] < EMPTY * 0.5
    src_totals = jnp.sum(is_valid.astype(jnp.int32), axis=1)
    offsets = jnp.cumsum(src_totals) - src_totals
    slot_pos = jnp.arange(capacity, dtype=jnp.int32)
    dest_rows = jnp.where(is_valid, offsets[:, None] + slot_pos[None, :], tok_rows)
    compact = (
        jnp.zeros((tok_rows, model_width), jnp.bfloat16)
        .at[dest_rows.reshape(-1)]
        .set(recv_rows.reshape(-1, model_width), mode="drop")
    )
    up_local = up_weight[0]
    down_local = down_weight[0]
    core = lax.axis_index("expert") % 2
    half = projection.shape[1] // 2
    own_cols = lax.dynamic_slice_in_dim(projection, core * half, half, 1)
    own_half = ring_gather(own_cols, dp_index, n_dp, experts)
    other_half = lax.ppermute(own_half, "expert", [(e, e ^ 1) for e in range(experts)])
    head = jnp.where(
        core == 0,
        jnp.concatenate([own_half, other_half], axis=1),
        jnp.concatenate([other_half, own_half], axis=1),
    )
    fold = jnp.dot(down_local, head, preferred_element_type=jnp.float32)
    fold_hi = fold.astype(jnp.bfloat16)
    fold_lo = (fold - fold_hi.astype(jnp.float32)).astype(jnp.bfloat16)
    hidden = jax.nn.gelu(
        jnp.dot(
            lax.all_gather(compact, "dp", axis=0, tiled=True),
            up_local,
            preferred_element_type=jnp.float32,
        ),
        approximate=False,
    ).astype(jnp.bfloat16)
    part_embed = jnp.dot(hidden, fold_hi, preferred_element_type=jnp.float32) + jnp.dot(
        hidden, fold_lo, preferred_element_type=jnp.float32
    )
    expert_out = lax.psum_scatter(
        part_embed.astype(jnp.bfloat16), "dp", scatter_dimension=0, tiled=True
    ).astype(jnp.float32)
    emb_width = expert_out.shape[1]
    slot_out = (
        jnp.take(expert_out, jnp.minimum(dest_rows, tok_rows - 1), axis=0) * is_valid[:, :, None]
    )
    returned = lax.all_to_all(
        slot_out.astype(jnp.bfloat16), "expert", split_axis=0, concat_axis=0, tiled=True
    ).astype(slot_out.dtype)
    token_out = jnp.take(returned.reshape(experts * capacity, emb_width), slot_ids, axis=0)
    ffn_pool = jnp.sum(token_out.reshape(samples_dev, PATCH, emb_width), axis=1)
    token_sum = jnp.sum(
        own_tokens.reshape(samples_dev, PATCH, model_width), axis=1, dtype=jnp.float32
    )
    own_mode = modality[:, 0]
    mode_ids = jnp.arange(mode_bias.shape[0], dtype=jnp.int32)
    mode_match = own_mode[:, None] == mode_ids[None, :]
    bias_rows = jnp.sum(jnp.where(mode_match[:, :, None], mode_bias[None, :, :], 0.0), axis=1)
    base = token_sum / PATCH + bias_rows
    own_embed = ffn_pool / PATCH + jnp.dot(
        base, head.astype(jnp.float32), precision=lax.Precision.HIGHEST
    )
    own_scale = jnp.sum(jnp.where(mode_match, logit_scale[None, :], 0.0), axis=1)
    own_target = pair_index[:, 0].astype(jnp.float32)
    meta_width = 128
    meta = jnp.concatenate(
        [
            jnp.broadcast_to(own_scale[:, None], (samples_dev, meta_width // 2)),
            jnp.broadcast_to(own_target[:, None], (samples_dev, meta_width // 2)),
        ],
        axis=1,
    )
    rows = jnp.concatenate([own_embed, meta], axis=1)
    got = lax.all_to_all(
        jnp.broadcast_to(rows[None], (n_dp,) + rows.shape), "dp", 0, 0, tiled=True
    ).reshape(n_dp * samples_dev, rows.shape[1])
    all_embed = got[:, :emb_width]
    all_scale = got[:, emb_width]
    all_target = got[:, emb_width + meta_width // 2].astype(jnp.int32)
    losses, emb_grads = losses_and_grads(all_embed, all_scale, all_target)
    row_start = dp_index * samples_dev
    own_loss = lax.dynamic_slice_in_dim(losses, row_start, samples_dev, 0)
    own_grad = lax.dynamic_slice_in_dim(emb_grads, row_start, samples_dev, 0)
    return (own_loss[:, None], own_grad[:, None, :])


def solution(mesh):
    placed = (
        P("dp", "expert", None),
        P("dp", "expert"),
        P("expert", None, "dp"),
        P("expert", "dp", None),
        P(),
        P("dp", None),
        P(),
        P("dp", "expert"),
        P("dp", "expert"),
    )
    return jax.shard_map(
        shards,
        mesh=mesh,
        in_specs=placed,
        out_specs=(P("dp", "expert"), P("dp", "expert", None)),
        check_vma=False,
    )
```

```python
import jax
import jax.numpy as jnp
from jax import lax
from jax.sharding import PartitionSpec as P

PATCH = 64
EMPTY = 64.0


def group_losses(raw_rows, anchor_scale, target_index):
    member_count = raw_rows.shape[0]
    norm_square = jnp.sum(raw_rows * raw_rows, axis=-1, keepdims=True)
    unit_rows = raw_rows / jnp.sqrt(norm_square + 1e-06)
    scores = anchor_scale[:, None] * jnp.dot(
        unit_rows, unit_rows.T, precision=lax.Precision.HIGHEST
    )
    member = jnp.arange(member_count, dtype=jnp.int32)
    is_self = member[:, None] == member[None, :]
    denominator = jnp.sum(jnp.where(is_self, 0.0, jnp.exp(scores)), axis=-1)
    positive = jnp.sum(jnp.where(member[None, :] == target_index[:, None], scores, 0.0), axis=-1)
    return jnp.log(denominator) - positive


def losses_and_grads(raw_rows, anchor_scale, target_index):
    losses, pullback = jax.vjp(
        lambda rows_in: group_losses(rows_in, anchor_scale, target_index), raw_rows
    )
    (row_grads,) = pullback(jnp.ones_like(losses))
    return (losses, row_grads)


def ring_gather(piece, dp_index, n_dp, experts):
    flip = experts // 2
    size = n_dp * experts
    up = []
    for d in range(n_dp):
        for e in range(experts):
            to = (d + 1, e) if d + 1 < n_dp else (0, e ^ flip)
            up.append((d * experts + e, to[0] * experts + to[1]))
    down = [(b, a) for a, b in up]
    assert len(set(b for _, b in up)) == size
    rows = piece.shape[0]
    out = jnp.zeros((n_dp, rows) + piece.shape[1:], piece.dtype)
    out = lax.dynamic_update_index_in_dim(out, piece, dp_index, 0)
    from_below = piece
    from_above = piece
    reach = n_dp // 2
    for step in range(1, reach):
        from_below = lax.ppermute(from_below, ("dp", "expert"), up)
        from_above = lax.ppermute(from_above, ("dp", "expert"), down)
        out = lax.dynamic_update_index_in_dim(out, from_below, (dp_index - step) % n_dp, 0)
        out = lax.dynamic_update_index_in_dim(out, from_above, (dp_index + step) % n_dp, 0)
    last_below = lax.ppermute(from_below[: rows // 2], ("dp", "expert"), up)
    last_above = lax.ppermute(from_above[rows // 2 :], ("dp", "expert"), down)
    last = jnp.concatenate([last_below, last_above], axis=0)
    out = lax.dynamic_update_index_in_dim(out, last, (dp_index + reach) % n_dp, 0)
    return out.reshape((n_dp * rows,) + piece.shape[1:])


def line_gather(piece, dp_index, n_dp):
    right = [(k, k + 1) for k in range(n_dp - 1)]
    left = [(k + 1, k) for k in range(n_dp - 1)]
    out = jnp.zeros((n_dp + 1,) + piece.shape, piece.dtype)
    out = lax.dynamic_update_index_in_dim(out, piece, dp_index, 0)
    from_left = piece
    from_right = piece
    for step in range(1, n_dp):
        from_left = lax.ppermute(from_left, "dp", right)
        from_right = lax.ppermute(from_right, "dp", left)
        at_left = jnp.where(dp_index - step >= 0, dp_index - step, n_dp)
        at_right = jnp.where(dp_index + step < n_dp, dp_index + step, n_dp)
        out = lax.dynamic_update_index_in_dim(out, from_left, at_left, 0)
        out = lax.dynamic_update_index_in_dim(out, from_right, at_right, 0)
    return out[:n_dp].reshape((n_dp * piece.shape[0],) + piece.shape[1:])


def shards(
    tokens,
    assignment,
    up_weight,
    down_weight,
    mode_bias,
    projection,
    logit_scale,
    modality,
    pair_index,
):
    tok_rows = tokens.shape[0]
    model_width = tokens.shape[2]
    experts = lax.axis_size("expert")
    n_dp = lax.axis_size("dp")
    capacity = 2 * tok_rows // experts
    samples_dev = tok_rows // PATCH
    dp_index = lax.axis_index("dp")
    own_tokens = tokens[:, 0, :]
    own_assign = assignment[:, 0]
    expert_ids = jnp.arange(experts, dtype=jnp.int32)
    one_hot = (own_assign[:, None] == expert_ids[None, :]).astype(jnp.int32)
    running = jnp.cumsum(one_hot, axis=0)
    rank_in = jnp.sum(one_hot * (running - 1), axis=1)
    slot_ids = own_assign * capacity + rank_in
    empty_rows = jnp.zeros((experts * capacity, model_width), jnp.bfloat16).at[:, 0].set(EMPTY)
    send_rows = empty_rows.at[slot_ids].set(own_tokens)
    send_rows = send_rows.reshape(experts, capacity, model_width)
    recv_rows = lax.all_to_all(send_rows, "expert", split_axis=0, concat_axis=0, tiled=True)
    is_valid = recv_rows[:, :, 0] < EMPTY * 0.5
    src_totals = jnp.sum(is_valid.astype(jnp.int32), axis=1)
    offsets = jnp.cumsum(src_totals) - src_totals
    slot_pos = jnp.arange(capacity, dtype=jnp.int32)
    dest_rows = jnp.where(is_valid, offsets[:, None] + slot_pos[None, :], tok_rows)
    compact = (
        jnp.zeros((tok_rows, model_width), jnp.bfloat16)
        .at[dest_rows.reshape(-1)]
        .set(recv_rows.reshape(-1, model_width), mode="drop")
    )
    up_local = up_weight[0]
    down_local = down_weight[0]
    core = lax.axis_index("expert") % 2
    half = projection.shape[1] // 2
    own_cols = lax.dynamic_slice_in_dim(projection, core * half, half, 1)
    own_half = ring_gather(own_cols, dp_index, n_dp, experts)
    other_half = lax.ppermute(own_half, "expert", [(e, e ^ 1) for e in range(experts)])
    head = jnp.where(
        core == 0,
        jnp.concatenate([own_half, other_half], axis=1),
        jnp.concatenate([other_half, own_half], axis=1),
    )
    fold = jnp.dot(down_local, head, preferred_element_type=jnp.float32)
    fold_hi = fold.astype(jnp.bfloat16)
    fold_lo = (fold - fold_hi.astype(jnp.float32)).astype(jnp.bfloat16)
    hidden = jax.nn.gelu(
        jnp.dot(
            line_gather(compact, dp_index, n_dp),
            up_local,
            preferred_element_type=jnp.float32,
        ),
        approximate=False,
    ).astype(jnp.bfloat16)
    part_embed = jnp.dot(hidden, fold_hi, preferred_element_type=jnp.float32) + jnp.dot(
        hidden, fold_lo, preferred_element_type=jnp.float32
    )
    expert_out = lax.psum_scatter(
        part_embed.astype(jnp.bfloat16), "dp", scatter_dimension=0, tiled=True
    ).astype(jnp.float32)
    emb_width = expert_out.shape[1]
    slot_out = (
        jnp.take(expert_out, jnp.minimum(dest_rows, tok_rows - 1), axis=0) * is_valid[:, :, None]
    )
    returned = lax.all_to_all(
        slot_out.astype(jnp.bfloat16), "expert", split_axis=0, concat_axis=0, tiled=True
    ).astype(slot_out.dtype)
    token_out = jnp.take(returned.reshape(experts * capacity, emb_width), slot_ids, axis=0)
    ffn_pool = jnp.sum(token_out.reshape(samples_dev, PATCH, emb_width), axis=1)
    token_sum = jnp.sum(
        own_tokens.reshape(samples_dev, PATCH, model_width), axis=1, dtype=jnp.float32
    )
    own_mode = modality[:, 0]
    mode_ids = jnp.arange(mode_bias.shape[0], dtype=jnp.int32)
    mode_match = own_mode[:, None] == mode_ids[None, :]
    bias_rows = jnp.sum(jnp.where(mode_match[:, :, None], mode_bias[None, :, :], 0.0), axis=1)
    base = token_sum / PATCH + bias_rows
    own_embed = ffn_pool / PATCH + jnp.dot(
        base, head.astype(jnp.float32), precision=lax.Precision.HIGHEST
    )
    own_scale = jnp.sum(jnp.where(mode_match, logit_scale[None, :], 0.0), axis=1)
    own_target = pair_index[:, 0].astype(jnp.float32)
    meta_width = 128
    meta = jnp.concatenate(
        [
            jnp.broadcast_to(own_scale[:, None], (samples_dev, meta_width // 2)),
            jnp.broadcast_to(own_target[:, None], (samples_dev, meta_width // 2)),
        ],
        axis=1,
    )
    rows = jnp.concatenate([own_embed, meta], axis=1)
    got = lax.all_to_all(
        jnp.broadcast_to(rows[None], (n_dp,) + rows.shape), "dp", 0, 0, tiled=True
    ).reshape(n_dp * samples_dev, rows.shape[1])
    all_embed = got[:, :emb_width]
    all_scale = got[:, emb_width]
    all_target = got[:, emb_width + meta_width // 2].astype(jnp.int32)
    losses, emb_grads = losses_and_grads(all_embed, all_scale, all_target)
    row_start = dp_index * samples_dev
    own_loss = lax.dynamic_slice_in_dim(losses, row_start, samples_dev, 0)
    own_grad = lax.dynamic_slice_in_dim(emb_grads, row_start, samples_dev, 0)
    return (own_loss[:, None], own_grad[:, None, :])


def solution(mesh):
    placed = (
        P("dp", "expert", None),
        P("dp", "expert"),
        P("expert", None, "dp"),
        P("expert", "dp", None),
        P(),
        P("dp", None),
        P(),
        P("dp", "expert"),
        P("dp", "expert"),
    )
    return jax.shard_map(
        shards,
        mesh=mesh,
        in_specs=placed,
        out_specs=(P("dp", "expert"), P("dp", "expert", None)),
        check_vma=False,
    )
```

```python
import jax
import jax.numpy as jnp
from jax import lax
from jax.sharding import PartitionSpec as P

PATCH = 64
EMPTY = 64.0


def group_losses(raw_rows, anchor_scale, target_index):
    member_count = raw_rows.shape[0]
    norm_square = jnp.sum(raw_rows * raw_rows, axis=-1, keepdims=True)
    unit_rows = raw_rows / jnp.sqrt(norm_square + 1e-06)
    scores = anchor_scale[:, None] * jnp.dot(
        unit_rows, unit_rows.T, precision=lax.Precision.HIGHEST
    )
    member = jnp.arange(member_count, dtype=jnp.int32)
    is_self = member[:, None] == member[None, :]
    denominator = jnp.sum(jnp.where(is_self, 0.0, jnp.exp(scores)), axis=-1)
    positive = jnp.sum(jnp.where(member[None, :] == target_index[:, None], scores, 0.0), axis=-1)
    return jnp.log(denominator) - positive


def losses_and_grads(raw_rows, anchor_scale, target_index):
    losses, pullback = jax.vjp(
        lambda rows_in: group_losses(rows_in, anchor_scale, target_index), raw_rows
    )
    (row_grads,) = pullback(jnp.ones_like(losses))
    return (losses, row_grads)


def ring_gather(piece, dp_index, n_dp, experts):
    flip = experts // 2
    size = n_dp * experts
    up = []
    for d in range(n_dp):
        for e in range(experts):
            to = (d + 1, e) if d + 1 < n_dp else (0, e ^ flip)
            up.append((d * experts + e, to[0] * experts + to[1]))
    down = [(b, a) for a, b in up]
    assert len(set(b for _, b in up)) == size
    rows = piece.shape[0]
    out = jnp.zeros((n_dp, rows) + piece.shape[1:], piece.dtype)
    out = lax.dynamic_update_index_in_dim(out, piece, dp_index, 0)
    from_below = piece
    from_above = piece
    reach = n_dp // 2
    for step in range(1, reach):
        from_below = lax.ppermute(from_below, ("dp", "expert"), up)
        from_above = lax.ppermute(from_above, ("dp", "expert"), down)
        out = lax.dynamic_update_index_in_dim(out, from_below, (dp_index - step) % n_dp, 0)
        out = lax.dynamic_update_index_in_dim(out, from_above, (dp_index + step) % n_dp, 0)
    last_below = lax.ppermute(from_below[: rows // 2], ("dp", "expert"), up)
    last_above = lax.ppermute(from_above[rows // 2 :], ("dp", "expert"), down)
    last = jnp.concatenate([last_below, last_above], axis=0)
    out = lax.dynamic_update_index_in_dim(out, last, (dp_index + reach) % n_dp, 0)
    return out.reshape((n_dp * rows,) + piece.shape[1:])


def shards(
    tokens,
    assignment,
    up_weight,
    down_weight,
    mode_bias,
    projection,
    logit_scale,
    modality,
    pair_index,
):
    tok_rows = tokens.shape[0]
    model_width = tokens.shape[2]
    experts = lax.axis_size("expert")
    n_dp = lax.axis_size("dp")
    capacity = 2 * tok_rows // experts
    samples_dev = tok_rows // PATCH
    dp_index = lax.axis_index("dp")
    own_tokens = tokens[:, 0, :]
    own_assign = assignment[:, 0]
    expert_ids = jnp.arange(experts, dtype=jnp.int32)
    one_hot = (own_assign[:, None] == expert_ids[None, :]).astype(jnp.int32)
    running = jnp.cumsum(one_hot, axis=0)
    rank_in = jnp.sum(one_hot * (running - 1), axis=1)
    slot_ids = own_assign * capacity + rank_in
    empty_rows = jnp.zeros((experts * capacity, model_width), jnp.bfloat16).at[:, 0].set(EMPTY)
    send_rows = empty_rows.at[slot_ids].set(own_tokens)
    send_rows = send_rows.reshape(experts, capacity, model_width)
    recv_rows = lax.all_to_all(send_rows, "expert", split_axis=0, concat_axis=0, tiled=True)
    is_valid = recv_rows[:, :, 0] < EMPTY * 0.5
    src_totals = jnp.sum(is_valid.astype(jnp.int32), axis=1)
    offsets = jnp.cumsum(src_totals) - src_totals
    slot_pos = jnp.arange(capacity, dtype=jnp.int32)
    dest_rows = jnp.where(is_valid, offsets[:, None] + slot_pos[None, :], tok_rows)
    compact = (
        jnp.zeros((tok_rows, model_width), jnp.bfloat16)
        .at[dest_rows.reshape(-1)]
        .set(recv_rows.reshape(-1, model_width), mode="drop")
    )
    up_local = up_weight[0]
    down_local = down_weight[0]
    e_idx = lax.axis_index("expert")
    ring_x = 4
    span = 2 * ring_x
    piece_rows = projection.shape[0] // span
    piece = lax.dynamic_slice_in_dim(projection, (e_idx % span) * piece_rows, piece_rows, 0)
    by_block = ring_gather(piece, dp_index, n_dp, experts).reshape(
        (n_dp, piece_rows) + projection.shape[1:]
    )
    core = e_idx % 2
    sibling = lax.ppermute(by_block, "expert", [(e, e ^ 1) for e in range(experts)])
    pair = jnp.where(
        core == 0, jnp.stack([by_block, sibling], axis=1), jnp.stack([sibling, by_block], axis=1)
    )
    x_pos = (e_idx // 2) % ring_x

    def shifted(e, step):
        return (e // span) * span + ((e // 2 + step) % ring_x) * 2 + e % 2

    to_right = [(e, shifted(e, 1)) for e in range(experts)]
    to_left = [(e, shifted(e, -1)) for e in range(experts)]
    from_left = lax.ppermute(pair, "expert", to_right)
    from_right = lax.ppermute(pair, "expert", to_left)
    far = jnp.concatenate(
        [
            lax.ppermute(from_left[: n_dp // 2], "expert", to_right),
            lax.ppermute(from_right[n_dp // 2 :], "expert", to_left),
        ],
        axis=0,
    )
    chips = jnp.zeros((ring_x,) + pair.shape, pair.dtype)
    chips = lax.dynamic_update_index_in_dim(chips, pair, x_pos, 0)
    chips = lax.dynamic_update_index_in_dim(chips, from_left, (x_pos - 1) % ring_x, 0)
    chips = lax.dynamic_update_index_in_dim(chips, from_right, (x_pos + 1) % ring_x, 0)
    chips = lax.dynamic_update_index_in_dim(chips, far, (x_pos + 2) % ring_x, 0)
    head = chips.transpose(1, 0, 2, 3, 4).reshape(projection.shape[0] * n_dp, projection.shape[1])
    fold = jnp.dot(down_local, head, preferred_element_type=jnp.float32)
    fold_hi = fold.astype(jnp.bfloat16)
    fold_lo = (fold - fold_hi.astype(jnp.float32)).astype(jnp.bfloat16)
    hidden = jax.nn.gelu(
        jnp.dot(
            lax.all_gather(compact, "dp", axis=0, tiled=True),
            up_local,
            preferred_element_type=jnp.float32,
        ),
        approximate=False,
    ).astype(jnp.bfloat16)
    part_embed = jnp.dot(hidden, fold_hi, preferred_element_type=jnp.float32) + jnp.dot(
        hidden, fold_lo, preferred_element_type=jnp.float32
    )
    expert_out = lax.psum_scatter(
        part_embed.astype(jnp.bfloat16), "dp", scatter_dimension=0, tiled=True
    ).astype(jnp.float32)
    emb_width = expert_out.shape[1]
    slot_out = (
        jnp.take(expert_out, jnp.minimum(dest_rows, tok_rows - 1), axis=0) * is_valid[:, :, None]
    )
    returned = lax.all_to_all(
        slot_out.astype(jnp.bfloat16), "expert", split_axis=0, concat_axis=0, tiled=True
    ).astype(slot_out.dtype)
    token_out = jnp.take(returned.reshape(experts * capacity, emb_width), slot_ids, axis=0)
    ffn_pool = jnp.sum(token_out.reshape(samples_dev, PATCH, emb_width), axis=1)
    token_sum = jnp.sum(
        own_tokens.reshape(samples_dev, PATCH, model_width), axis=1, dtype=jnp.float32
    )
    own_mode = modality[:, 0]
    mode_ids = jnp.arange(mode_bias.shape[0], dtype=jnp.int32)
    mode_match = own_mode[:, None] == mode_ids[None, :]
    bias_rows = jnp.sum(jnp.where(mode_match[:, :, None], mode_bias[None, :, :], 0.0), axis=1)
    base = token_sum / PATCH + bias_rows
    own_embed = ffn_pool / PATCH + jnp.dot(
        base, head.astype(jnp.float32), precision=lax.Precision.HIGHEST
    )
    own_scale = jnp.sum(jnp.where(mode_match, logit_scale[None, :], 0.0), axis=1)
    own_target = pair_index[:, 0].astype(jnp.float32)
    meta_width = 128
    meta = jnp.concatenate(
        [
            jnp.broadcast_to(own_scale[:, None], (samples_dev, meta_width // 2)),
            jnp.broadcast_to(own_target[:, None], (samples_dev, meta_width // 2)),
        ],
        axis=1,
    )
    rows = jnp.concatenate([own_embed, meta], axis=1)
    got = lax.all_to_all(
        jnp.broadcast_to(rows[None], (n_dp,) + rows.shape), "dp", 0, 0, tiled=True
    ).reshape(n_dp * samples_dev, rows.shape[1])
    all_embed = got[:, :emb_width]
    all_scale = got[:, emb_width]
    all_target = got[:, emb_width + meta_width // 2].astype(jnp.int32)
    losses, emb_grads = losses_and_grads(all_embed, all_scale, all_target)
    row_start = dp_index * samples_dev
    own_loss = lax.dynamic_slice_in_dim(losses, row_start, samples_dev, 0)
    own_grad = lax.dynamic_slice_in_dim(emb_grads, row_start, samples_dev, 0)
    return (own_loss[:, None], own_grad[:, None, :])


def solution(mesh):
    placed = (
        P("dp", "expert", None),
        P("dp", "expert"),
        P("expert", None, "dp"),
        P("expert", "dp", None),
        P(),
        P("dp", None),
        P(),
        P("dp", "expert"),
        P("dp", "expert"),
    )
    return jax.shard_map(
        shards,
        mesh=mesh,
        in_specs=placed,
        out_specs=(P("dp", "expert"), P("dp", "expert", None)),
        check_vma=False,
    )
```

```python
import jax
import jax.numpy as jnp
from jax import lax
from jax.sharding import PartitionSpec as P

PATCH = 64
EMPTY = 64.0


def group_losses(raw_rows, anchor_scale, target_index):
    member_count = raw_rows.shape[0]
    norm_square = jnp.sum(raw_rows * raw_rows, axis=-1, keepdims=True)
    unit_rows = raw_rows / jnp.sqrt(norm_square + 1e-06)
    scores = anchor_scale[:, None] * jnp.dot(
        unit_rows, unit_rows.T, precision=lax.Precision.HIGHEST
    )
    member = jnp.arange(member_count, dtype=jnp.int32)
    is_self = member[:, None] == member[None, :]
    denominator = jnp.sum(jnp.where(is_self, 0.0, jnp.exp(scores)), axis=-1)
    positive = jnp.sum(jnp.where(member[None, :] == target_index[:, None], scores, 0.0), axis=-1)
    return jnp.log(denominator) - positive


def losses_and_grads(raw_rows, anchor_scale, target_index):
    losses, pullback = jax.vjp(
        lambda rows_in: group_losses(rows_in, anchor_scale, target_index), raw_rows
    )
    (row_grads,) = pullback(jnp.ones_like(losses))
    return (losses, row_grads)


def ring_gather(piece, dp_index, n_dp, experts):
    flip = experts // 2
    size = n_dp * experts
    up = []
    for d in range(n_dp):
        for e in range(experts):
            to = (d + 1, e) if d + 1 < n_dp else (0, e ^ flip)
            up.append((d * experts + e, to[0] * experts + to[1]))
    down = [(b, a) for a, b in up]
    assert len(set(b for _, b in up)) == size
    rows = piece.shape[0]
    out = jnp.zeros((n_dp, rows) + piece.shape[1:], piece.dtype)
    out = lax.dynamic_update_index_in_dim(out, piece, dp_index, 0)
    from_below = piece
    from_above = piece
    reach = n_dp // 2
    for step in range(1, reach):
        from_below = lax.ppermute(from_below, ("dp", "expert"), up)
        from_above = lax.ppermute(from_above, ("dp", "expert"), down)
        out = lax.dynamic_update_index_in_dim(out, from_below, (dp_index - step) % n_dp, 0)
        out = lax.dynamic_update_index_in_dim(out, from_above, (dp_index + step) % n_dp, 0)
    last_below = lax.ppermute(from_below[: rows // 2], ("dp", "expert"), up)
    last_above = lax.ppermute(from_above[rows // 2 :], ("dp", "expert"), down)
    last = jnp.concatenate([last_below, last_above], axis=0)
    out = lax.dynamic_update_index_in_dim(out, last, (dp_index + reach) % n_dp, 0)
    return out.reshape((n_dp * rows,) + piece.shape[1:])


def line_gather(piece, dp_index, n_dp):
    right = [(k, k + 1) for k in range(n_dp - 1)]
    left = [(k + 1, k) for k in range(n_dp - 1)]
    out = jnp.zeros((n_dp + 1,) + piece.shape, piece.dtype)
    out = lax.dynamic_update_index_in_dim(out, piece, dp_index, 0)
    from_left = piece
    from_right = piece
    for step in range(1, n_dp):
        from_left = lax.ppermute(from_left, "dp", right)
        from_right = lax.ppermute(from_right, "dp", left)
        at_left = jnp.where(dp_index - step >= 0, dp_index - step, n_dp)
        at_right = jnp.where(dp_index + step < n_dp, dp_index + step, n_dp)
        out = lax.dynamic_update_index_in_dim(out, from_left, at_left, 0)
        out = lax.dynamic_update_index_in_dim(out, from_right, at_right, 0)
    return out[:n_dp].reshape((n_dp * piece.shape[0],) + piece.shape[1:])


def shards(
    tokens,
    assignment,
    up_weight,
    down_weight,
    mode_bias,
    projection,
    logit_scale,
    modality,
    pair_index,
):
    tok_rows = tokens.shape[0]
    model_width = tokens.shape[2]
    experts = lax.axis_size("expert")
    n_dp = lax.axis_size("dp")
    capacity = 2 * tok_rows // experts
    samples_dev = tok_rows // PATCH
    dp_index = lax.axis_index("dp")
    own_tokens = tokens[:, 0, :]
    own_assign = assignment[:, 0]
    expert_ids = jnp.arange(experts, dtype=jnp.int32)
    one_hot = (own_assign[:, None] == expert_ids[None, :]).astype(jnp.int32)
    running = jnp.cumsum(one_hot, axis=0)
    rank_in = jnp.sum(one_hot * (running - 1), axis=1)
    slot_ids = own_assign * capacity + rank_in
    empty_rows = jnp.zeros((experts * capacity, model_width), jnp.bfloat16).at[:, 0].set(EMPTY)
    send_rows = empty_rows.at[slot_ids].set(own_tokens)
    send_rows = send_rows.reshape(experts, capacity, model_width)
    recv_rows = lax.all_to_all(send_rows, "expert", split_axis=0, concat_axis=0, tiled=True)
    is_valid = recv_rows[:, :, 0] < EMPTY * 0.5
    src_totals = jnp.sum(is_valid.astype(jnp.int32), axis=1)
    offsets = jnp.cumsum(src_totals) - src_totals
    slot_pos = jnp.arange(capacity, dtype=jnp.int32)
    dest_rows = jnp.where(is_valid, offsets[:, None] + slot_pos[None, :], tok_rows)
    compact = (
        jnp.zeros((tok_rows, model_width), jnp.bfloat16)
        .at[dest_rows.reshape(-1)]
        .set(recv_rows.reshape(-1, model_width), mode="drop")
    )
    up_local = up_weight[0]
    down_local = down_weight[0]
    e_idx = lax.axis_index("expert")
    ring_x = 4
    span = 2 * ring_x
    piece_rows = projection.shape[0] // span
    piece = lax.dynamic_slice_in_dim(projection, (e_idx % span) * piece_rows, piece_rows, 0)
    piece, compact = lax.optimization_barrier((piece, compact))
    by_block = ring_gather(piece, dp_index, n_dp, experts).reshape(
        (n_dp, piece_rows) + projection.shape[1:]
    )
    core = e_idx % 2
    sibling = lax.ppermute(by_block, "expert", [(e, e ^ 1) for e in range(experts)])
    pair = jnp.where(
        core == 0, jnp.stack([by_block, sibling], axis=1), jnp.stack([sibling, by_block], axis=1)
    )
    x_pos = (e_idx // 2) % ring_x

    def shifted(e, step):
        return (e // span) * span + ((e // 2 + step) % ring_x) * 2 + e % 2

    to_right = [(e, shifted(e, 1)) for e in range(experts)]
    to_left = [(e, shifted(e, -1)) for e in range(experts)]
    from_left = lax.ppermute(pair, "expert", to_right)
    from_right = lax.ppermute(pair, "expert", to_left)
    far = jnp.concatenate(
        [
            lax.ppermute(from_left[: n_dp // 2], "expert", to_right),
            lax.ppermute(from_right[n_dp // 2 :], "expert", to_left),
        ],
        axis=0,
    )
    chips = jnp.zeros((ring_x,) + pair.shape, pair.dtype)
    chips = lax.dynamic_update_index_in_dim(chips, pair, x_pos, 0)
    chips = lax.dynamic_update_index_in_dim(chips, from_left, (x_pos - 1) % ring_x, 0)
    chips = lax.dynamic_update_index_in_dim(chips, from_right, (x_pos + 1) % ring_x, 0)
    chips = lax.dynamic_update_index_in_dim(chips, far, (x_pos + 2) % ring_x, 0)
    head = chips.transpose(1, 0, 2, 3, 4).reshape(projection.shape[0] * n_dp, projection.shape[1])
    fold = jnp.dot(down_local, head, preferred_element_type=jnp.float32)
    fold_hi = fold.astype(jnp.bfloat16)
    fold_lo = (fold - fold_hi.astype(jnp.float32)).astype(jnp.bfloat16)
    hidden = jax.nn.gelu(
        jnp.dot(
            line_gather(compact, dp_index, n_dp),
            up_local,
            preferred_element_type=jnp.float32,
        ),
        approximate=False,
    ).astype(jnp.bfloat16)
    part_embed = jnp.dot(hidden, fold_hi, preferred_element_type=jnp.float32) + jnp.dot(
        hidden, fold_lo, preferred_element_type=jnp.float32
    )
    expert_out = lax.psum_scatter(
        part_embed.astype(jnp.bfloat16), "dp", scatter_dimension=0, tiled=True
    ).astype(jnp.float32)
    emb_width = expert_out.shape[1]
    slot_out = (
        jnp.take(expert_out, jnp.minimum(dest_rows, tok_rows - 1), axis=0) * is_valid[:, :, None]
    )
    returned = lax.all_to_all(
        slot_out.astype(jnp.bfloat16), "expert", split_axis=0, concat_axis=0, tiled=True
    ).astype(slot_out.dtype)
    token_out = jnp.take(returned.reshape(experts * capacity, emb_width), slot_ids, axis=0)
    ffn_pool = jnp.sum(token_out.reshape(samples_dev, PATCH, emb_width), axis=1)
    token_sum = jnp.sum(
        own_tokens.reshape(samples_dev, PATCH, model_width), axis=1, dtype=jnp.float32
    )
    own_mode = modality[:, 0]
    mode_ids = jnp.arange(mode_bias.shape[0], dtype=jnp.int32)
    mode_match = own_mode[:, None] == mode_ids[None, :]
    bias_rows = jnp.sum(jnp.where(mode_match[:, :, None], mode_bias[None, :, :], 0.0), axis=1)
    base = token_sum / PATCH + bias_rows
    own_embed = ffn_pool / PATCH + jnp.dot(
        base, head.astype(jnp.float32), precision=lax.Precision.HIGHEST
    )
    own_scale = jnp.sum(jnp.where(mode_match, logit_scale[None, :], 0.0), axis=1)
    own_target = pair_index[:, 0].astype(jnp.float32)
    meta_width = 128
    meta = jnp.concatenate(
        [
            jnp.broadcast_to(own_scale[:, None], (samples_dev, meta_width // 2)),
            jnp.broadcast_to(own_target[:, None], (samples_dev, meta_width // 2)),
        ],
        axis=1,
    )
    rows = jnp.concatenate([own_embed, meta], axis=1)
    got = lax.all_to_all(
        jnp.broadcast_to(rows[None], (n_dp,) + rows.shape), "dp", 0, 0, tiled=True
    ).reshape(n_dp * samples_dev, rows.shape[1])
    all_embed = got[:, :emb_width]
    all_scale = got[:, emb_width]
    all_target = got[:, emb_width + meta_width // 2].astype(jnp.int32)
    losses, emb_grads = losses_and_grads(all_embed, all_scale, all_target)
    row_start = dp_index * samples_dev
    own_loss = lax.dynamic_slice_in_dim(losses, row_start, samples_dev, 0)
    own_grad = lax.dynamic_slice_in_dim(emb_grads, row_start, samples_dev, 0)
    return (own_loss[:, None], own_grad[:, None, :])


def solution(mesh):
    placed = (
        P("dp", "expert", None),
        P("dp", "expert"),
        P("expert", None, "dp"),
        P("expert", "dp", None),
        P(),
        P("dp", None),
        P(),
        P("dp", "expert"),
        P("dp", "expert"),
    )
    return jax.shard_map(
        shards,
        mesh=mesh,
        in_specs=placed,
        out_specs=(P("dp", "expert"), P("dp", "expert", None)),
        check_vma=False,
    )
```

```python
import jax
import jax.numpy as jnp
from jax import lax
from jax.sharding import PartitionSpec as P

PATCH = 64
EMPTY = 64.0


def group_losses(raw_rows, anchor_scale, target_index):
    member_count = raw_rows.shape[0]
    norm_square = jnp.sum(raw_rows * raw_rows, axis=-1, keepdims=True)
    unit_rows = raw_rows / jnp.sqrt(norm_square + 1e-06)
    scores = anchor_scale[:, None] * jnp.dot(
        unit_rows, unit_rows.T, precision=lax.Precision.HIGHEST
    )
    member = jnp.arange(member_count, dtype=jnp.int32)
    is_self = member[:, None] == member[None, :]
    denominator = jnp.sum(jnp.where(is_self, 0.0, jnp.exp(scores)), axis=-1)
    positive = jnp.sum(jnp.where(member[None, :] == target_index[:, None], scores, 0.0), axis=-1)
    return jnp.log(denominator) - positive


def losses_and_grads(raw_rows, anchor_scale, target_index):
    losses, pullback = jax.vjp(
        lambda rows_in: group_losses(rows_in, anchor_scale, target_index), raw_rows
    )
    (row_grads,) = pullback(jnp.ones_like(losses))
    return (losses, row_grads)


def ring_gather(piece, dp_index, n_dp, experts):
    flip = experts // 2
    size = n_dp * experts
    up = []
    for d in range(n_dp):
        for e in range(experts):
            to = (d + 1, e) if d + 1 < n_dp else (0, e ^ flip)
            up.append((d * experts + e, to[0] * experts + to[1]))
    down = [(b, a) for a, b in up]
    assert len(set(b for _, b in up)) == size
    rows = piece.shape[0]
    out = jnp.zeros((n_dp, rows) + piece.shape[1:], piece.dtype)
    out = lax.dynamic_update_index_in_dim(out, piece, dp_index, 0)
    from_below = piece
    from_above = piece
    reach = n_dp // 2
    for step in range(1, reach):
        from_below = lax.ppermute(from_below, ("dp", "expert"), up)
        from_above = lax.ppermute(from_above, ("dp", "expert"), down)
        out = lax.dynamic_update_index_in_dim(out, from_below, (dp_index - step) % n_dp, 0)
        out = lax.dynamic_update_index_in_dim(out, from_above, (dp_index + step) % n_dp, 0)
    last_below = lax.ppermute(from_below[: rows // 2], ("dp", "expert"), up)
    last_above = lax.ppermute(from_above[rows // 2 :], ("dp", "expert"), down)
    last = jnp.concatenate([last_below, last_above], axis=0)
    out = lax.dynamic_update_index_in_dim(out, last, (dp_index + reach) % n_dp, 0)
    return out.reshape((n_dp * rows,) + piece.shape[1:])


def shards(
    tokens,
    assignment,
    up_weight,
    down_weight,
    mode_bias,
    projection,
    logit_scale,
    modality,
    pair_index,
):
    tok_rows = tokens.shape[0]
    model_width = tokens.shape[2]
    experts = lax.axis_size("expert")
    n_dp = lax.axis_size("dp")
    capacity = 2 * tok_rows // experts
    samples_dev = tok_rows // PATCH
    dp_index = lax.axis_index("dp")
    own_tokens = tokens[:, 0, :]
    own_assign = assignment[:, 0]
    expert_ids = jnp.arange(experts, dtype=jnp.int32)
    one_hot = (own_assign[:, None] == expert_ids[None, :]).astype(jnp.int32)
    running = jnp.cumsum(one_hot, axis=0)
    rank_in = jnp.sum(one_hot * (running - 1), axis=1)
    slot_ids = own_assign * capacity + rank_in
    empty_rows = jnp.zeros((experts * capacity, model_width), jnp.bfloat16).at[:, 0].set(EMPTY)
    send_rows = empty_rows.at[slot_ids].set(own_tokens)
    send_rows = send_rows.reshape(experts, capacity, model_width)
    split = model_width // 2
    recv_a = lax.all_to_all(send_rows[:, :, :split], "expert", split_axis=0, concat_axis=0, tiled=True)
    is_valid = recv_a[:, :, 0] < EMPTY * 0.5
    src_totals = jnp.sum(is_valid.astype(jnp.int32), axis=1)
    offsets = jnp.cumsum(src_totals) - src_totals
    slot_pos = jnp.arange(capacity, dtype=jnp.int32)
    dest_rows = jnp.where(is_valid, offsets[:, None] + slot_pos[None, :], tok_rows)

    def compacted(rows):
        width = rows.shape[-1]
        return (
            jnp.zeros((tok_rows, width), jnp.bfloat16)
            .at[dest_rows.reshape(-1)]
            .set(rows.reshape(-1, width), mode="drop")
        )

    compact_a = compacted(recv_a)
    gathered_a = lax.all_gather(compact_a, "dp", axis=0, tiled=True)
    send_b, compact_a = lax.optimization_barrier((send_rows[:, :, split:], compact_a))
    recv_b = lax.all_to_all(send_b, "expert", split_axis=0, concat_axis=0, tiled=True)
    gathered_b = lax.all_gather(compacted(recv_b), "dp", axis=0, tiled=True)
    up_local = up_weight[0]
    down_local = down_weight[0]
    e_idx = lax.axis_index("expert")
    ring_x = 4
    span = 2 * ring_x
    piece_rows = projection.shape[0] // span
    piece = lax.dynamic_slice_in_dim(projection, (e_idx % span) * piece_rows, piece_rows, 0)
    by_block = ring_gather(piece, dp_index, n_dp, experts).reshape(
        (n_dp, piece_rows) + projection.shape[1:]
    )
    core = e_idx % 2
    sibling = lax.ppermute(by_block, "expert", [(e, e ^ 1) for e in range(experts)])
    pair = jnp.where(
        core == 0, jnp.stack([by_block, sibling], axis=1), jnp.stack([sibling, by_block], axis=1)
    )
    x_pos = (e_idx // 2) % ring_x

    def shifted(e, step):
        return (e // span) * span + ((e // 2 + step) % ring_x) * 2 + e % 2

    to_right = [(e, shifted(e, 1)) for e in range(experts)]
    to_left = [(e, shifted(e, -1)) for e in range(experts)]
    from_left = lax.ppermute(pair, "expert", to_right)
    from_right = lax.ppermute(pair, "expert", to_left)
    far = jnp.concatenate(
        [
            lax.ppermute(from_left[: n_dp // 2], "expert", to_right),
            lax.ppermute(from_right[n_dp // 2 :], "expert", to_left),
        ],
        axis=0,
    )
    chips = jnp.zeros((ring_x,) + pair.shape, pair.dtype)
    chips = lax.dynamic_update_index_in_dim(chips, pair, x_pos, 0)
    chips = lax.dynamic_update_index_in_dim(chips, from_left, (x_pos - 1) % ring_x, 0)
    chips = lax.dynamic_update_index_in_dim(chips, from_right, (x_pos + 1) % ring_x, 0)
    chips = lax.dynamic_update_index_in_dim(chips, far, (x_pos + 2) % ring_x, 0)
    head = chips.transpose(1, 0, 2, 3, 4).reshape(projection.shape[0] * n_dp, projection.shape[1])
    fold = jnp.dot(down_local, head, preferred_element_type=jnp.float32)
    fold_hi = fold.astype(jnp.bfloat16)
    fold_lo = (fold - fold_hi.astype(jnp.float32)).astype(jnp.bfloat16)
    hidden = jax.nn.gelu(
        jnp.dot(gathered_a, up_local[:split], preferred_element_type=jnp.float32)
        + jnp.dot(gathered_b, up_local[split:], preferred_element_type=jnp.float32),
        approximate=False,
    ).astype(jnp.bfloat16)
    part_embed = jnp.dot(hidden, fold_hi, preferred_element_type=jnp.float32) + jnp.dot(
        hidden, fold_lo, preferred_element_type=jnp.float32
    )
    expert_out = lax.psum_scatter(
        part_embed.astype(jnp.bfloat16), "dp", scatter_dimension=0, tiled=True
    ).astype(jnp.float32)
    emb_width = expert_out.shape[1]
    slot_out = (
        jnp.take(expert_out, jnp.minimum(dest_rows, tok_rows - 1), axis=0) * is_valid[:, :, None]
    )
    returned = lax.all_to_all(
        slot_out.astype(jnp.bfloat16), "expert", split_axis=0, concat_axis=0, tiled=True
    ).astype(slot_out.dtype)
    token_out = jnp.take(returned.reshape(experts * capacity, emb_width), slot_ids, axis=0)
    ffn_pool = jnp.sum(token_out.reshape(samples_dev, PATCH, emb_width), axis=1)
    token_sum = jnp.sum(
        own_tokens.reshape(samples_dev, PATCH, model_width), axis=1, dtype=jnp.float32
    )
    own_mode = modality[:, 0]
    mode_ids = jnp.arange(mode_bias.shape[0], dtype=jnp.int32)
    mode_match = own_mode[:, None] == mode_ids[None, :]
    bias_rows = jnp.sum(jnp.where(mode_match[:, :, None], mode_bias[None, :, :], 0.0), axis=1)
    base = token_sum / PATCH + bias_rows
    own_embed = ffn_pool / PATCH + jnp.dot(
        base, head.astype(jnp.float32), precision=lax.Precision.HIGHEST
    )
    own_scale = jnp.sum(jnp.where(mode_match, logit_scale[None, :], 0.0), axis=1)
    own_target = pair_index[:, 0].astype(jnp.float32)
    meta_width = 128
    meta = jnp.concatenate(
        [
            jnp.broadcast_to(own_scale[:, None], (samples_dev, meta_width // 2)),
            jnp.broadcast_to(own_target[:, None], (samples_dev, meta_width // 2)),
        ],
        axis=1,
    )
    rows = jnp.concatenate([own_embed, meta], axis=1)
    got = lax.all_to_all(
        jnp.broadcast_to(rows[None], (n_dp,) + rows.shape), "dp", 0, 0, tiled=True
    ).reshape(n_dp * samples_dev, rows.shape[1])
    all_embed = got[:, :emb_width]
    all_scale = got[:, emb_width]
    all_target = got[:, emb_width + meta_width // 2].astype(jnp.int32)
    losses, emb_grads = losses_and_grads(all_embed, all_scale, all_target)
    row_start = dp_index * samples_dev
    own_loss = lax.dynamic_slice_in_dim(losses, row_start, samples_dev, 0)
    own_grad = lax.dynamic_slice_in_dim(emb_grads, row_start, samples_dev, 0)
    return (own_loss[:, None], own_grad[:, None, :])


def solution(mesh):
    placed = (
        P("dp", "expert", None),
        P("dp", "expert"),
        P("expert", None, "dp"),
        P("expert", "dp", None),
        P(),
        P("dp", None),
        P(),
        P("dp", "expert"),
        P("dp", "expert"),
    )
    return jax.shard_map(
        shards,
        mesh=mesh,
        in_specs=placed,
        out_specs=(P("dp", "expert"), P("dp", "expert", None)),
        check_vma=False,
    )
```

```python
import jax
import jax.numpy as jnp
from jax import lax
from jax.sharding import PartitionSpec as P

PATCH = 64
EMPTY = 64.0


def group_losses(raw_rows, anchor_scale, target_index):
    member_count = raw_rows.shape[0]
    norm_square = jnp.sum(raw_rows * raw_rows, axis=-1, keepdims=True)
    unit_rows = raw_rows / jnp.sqrt(norm_square + 1e-06)
    scores = anchor_scale[:, None] * jnp.dot(
        unit_rows, unit_rows.T, precision=lax.Precision.HIGHEST
    )
    member = jnp.arange(member_count, dtype=jnp.int32)
    is_self = member[:, None] == member[None, :]
    denominator = jnp.sum(jnp.where(is_self, 0.0, jnp.exp(scores)), axis=-1)
    positive = jnp.sum(jnp.where(member[None, :] == target_index[:, None], scores, 0.0), axis=-1)
    return jnp.log(denominator) - positive


def losses_and_grads(raw_rows, anchor_scale, target_index):
    losses, pullback = jax.vjp(
        lambda rows_in: group_losses(rows_in, anchor_scale, target_index), raw_rows
    )
    (row_grads,) = pullback(jnp.ones_like(losses))
    return (losses, row_grads)


def ring_gather(piece, dp_index, n_dp, experts):
    flip = experts // 2
    size = n_dp * experts
    up = []
    for d in range(n_dp):
        for e in range(experts):
            to = (d + 1, e) if d + 1 < n_dp else (0, e ^ flip)
            up.append((d * experts + e, to[0] * experts + to[1]))
    down = [(b, a) for a, b in up]
    assert len(set(b for _, b in up)) == size
    rows = piece.shape[0]
    out = jnp.zeros((n_dp, rows) + piece.shape[1:], piece.dtype)
    out = lax.dynamic_update_index_in_dim(out, piece, dp_index, 0)
    from_below = piece
    from_above = piece
    reach = n_dp // 2
    for step in range(1, reach):
        from_below = lax.ppermute(from_below, ("dp", "expert"), up)
        from_above = lax.ppermute(from_above, ("dp", "expert"), down)
        out = lax.dynamic_update_index_in_dim(out, from_below, (dp_index - step) % n_dp, 0)
        out = lax.dynamic_update_index_in_dim(out, from_above, (dp_index + step) % n_dp, 0)
    last_below = lax.ppermute(from_below[: rows // 2], ("dp", "expert"), up)
    last_above = lax.ppermute(from_above[rows // 2 :], ("dp", "expert"), down)
    last = jnp.concatenate([last_below, last_above], axis=0)
    out = lax.dynamic_update_index_in_dim(out, last, (dp_index + reach) % n_dp, 0)
    return out.reshape((n_dp * rows,) + piece.shape[1:])


def ring_flood(arr, e_idx, experts, stride, ring):
    pos = (e_idx // stride) % ring

    def moved(e, step):
        digit = (e // stride) % ring
        return e + (((digit + step) % ring) - digit) * stride

    right = [(e, moved(e, 1)) for e in range(experts)]
    left = [(e, moved(e, -1)) for e in range(experts)]
    from_left = lax.ppermute(arr, "expert", right)
    from_right = lax.ppermute(arr, "expert", left)
    half = arr.shape[0] // 2
    far = jnp.concatenate(
        [
            lax.ppermute(from_left[:half], "expert", right),
            lax.ppermute(from_right[half:], "expert", left),
        ],
        axis=0,
    )
    out = jnp.zeros((ring,) + arr.shape, arr.dtype)
    out = lax.dynamic_update_index_in_dim(out, arr, pos, 0)
    out = lax.dynamic_update_index_in_dim(out, from_left, (pos - 1) % ring, 0)
    out = lax.dynamic_update_index_in_dim(out, from_right, (pos + 1) % ring, 0)
    out = lax.dynamic_update_index_in_dim(out, far, (pos + 2) % ring, 0)
    return out


def shards(
    tokens,
    assignment,
    up_weight,
    down_weight,
    mode_bias,
    projection,
    logit_scale,
    modality,
    pair_index,
):
    tok_rows = tokens.shape[0]
    model_width = tokens.shape[2]
    experts = lax.axis_size("expert")
    n_dp = lax.axis_size("dp")
    capacity = 2 * tok_rows // experts
    samples_dev = tok_rows // PATCH
    dp_index = lax.axis_index("dp")
    own_tokens = tokens[:, 0, :]
    own_assign = assignment[:, 0]
    expert_ids = jnp.arange(experts, dtype=jnp.int32)
    one_hot = (own_assign[:, None] == expert_ids[None, :]).astype(jnp.int32)
    running = jnp.cumsum(one_hot, axis=0)
    rank_in = jnp.sum(one_hot * (running - 1), axis=1)
    slot_ids = own_assign * capacity + rank_in
    empty_rows = jnp.zeros((experts * capacity, model_width), jnp.bfloat16).at[:, 0].set(EMPTY)
    send_rows = empty_rows.at[slot_ids].set(own_tokens)
    send_rows = send_rows.reshape(experts, capacity, model_width)
    recv_rows = lax.all_to_all(send_rows, "expert", split_axis=0, concat_axis=0, tiled=True)
    is_valid = recv_rows[:, :, 0] < EMPTY * 0.5
    src_totals = jnp.sum(is_valid.astype(jnp.int32), axis=1)
    offsets = jnp.cumsum(src_totals) - src_totals
    slot_pos = jnp.arange(capacity, dtype=jnp.int32)
    dest_rows = jnp.where(is_valid, offsets[:, None] + slot_pos[None, :], tok_rows)
    compact = (
        jnp.zeros((tok_rows, model_width), jnp.bfloat16)
        .at[dest_rows.reshape(-1)]
        .set(recv_rows.reshape(-1, model_width), mode="drop")
    )
    up_local = up_weight[0]
    down_local = down_weight[0]
    e_idx = lax.axis_index("expert")
    ring = 4
    plane = 2 * ring * ring
    piece_rows = projection.shape[0] // plane
    piece = lax.dynamic_slice_in_dim(projection, (e_idx % plane) * piece_rows, piece_rows, 0)
    by_block = ring_gather(piece, dp_index, n_dp, experts).reshape(
        (n_dp, piece_rows) + projection.shape[1:]
    )
    core = e_idx % 2
    sibling = lax.ppermute(by_block, "expert", [(e, e ^ 1) for e in range(experts)])
    pair = jnp.where(
        core == 0, jnp.stack([by_block, sibling], axis=1), jnp.stack([sibling, by_block], axis=1)
    )
    along_x = ring_flood(pair, e_idx, experts, 2, ring)
    along_y = ring_flood(along_x.transpose(1, 0, 2, 3, 4), e_idx, experts, 2 * ring, ring)
    head = along_y.transpose(1, 0, 2, 3, 4, 5).reshape(
        projection.shape[0] * n_dp, projection.shape[1]
    )
    fold = jnp.dot(down_local, head, preferred_element_type=jnp.float32)
    fold_hi = fold.astype(jnp.bfloat16)
    fold_lo = (fold - fold_hi.astype(jnp.float32)).astype(jnp.bfloat16)
    token_sum = jnp.sum(
        own_tokens.reshape(samples_dev, PATCH, model_width), axis=1, dtype=jnp.float32
    )
    own_mode = modality[:, 0]
    mode_ids = jnp.arange(mode_bias.shape[0], dtype=jnp.int32)
    mode_match = own_mode[:, None] == mode_ids[None, :]
    bias_rows = jnp.sum(jnp.where(mode_match[:, :, None], mode_bias[None, :, :], 0.0), axis=1)
    base = token_sum / PATCH + bias_rows
    base_embed = jnp.dot(base, head.astype(jnp.float32), precision=lax.Precision.HIGHEST)
    base_embed, fold_hi, fold_lo = lax.optimization_barrier((base_embed, fold_hi, fold_lo))
    hidden = jax.nn.gelu(
        jnp.dot(
            lax.all_gather(compact, "dp", axis=0, tiled=True),
            up_local,
            preferred_element_type=jnp.float32,
        ),
        approximate=False,
    ).astype(jnp.bfloat16)
    part_embed = jnp.dot(hidden, fold_hi, preferred_element_type=jnp.float32) + jnp.dot(
        hidden, fold_lo, preferred_element_type=jnp.float32
    )
    expert_out = lax.psum_scatter(
        part_embed.astype(jnp.bfloat16), "dp", scatter_dimension=0, tiled=True
    ).astype(jnp.float32)
    emb_width = expert_out.shape[1]
    slot_out = (
        jnp.take(expert_out, jnp.minimum(dest_rows, tok_rows - 1), axis=0) * is_valid[:, :, None]
    )
    returned = lax.all_to_all(
        slot_out.astype(jnp.bfloat16), "expert", split_axis=0, concat_axis=0, tiled=True
    ).astype(slot_out.dtype)
    token_out = jnp.take(returned.reshape(experts * capacity, emb_width), slot_ids, axis=0)
    ffn_pool = jnp.sum(token_out.reshape(samples_dev, PATCH, emb_width), axis=1)
    own_embed = ffn_pool / PATCH + base_embed
    own_scale = jnp.sum(jnp.where(mode_match, logit_scale[None, :], 0.0), axis=1)
    own_target = pair_index[:, 0].astype(jnp.float32)
    meta_width = 128
    meta = jnp.concatenate(
        [
            jnp.broadcast_to(own_scale[:, None], (samples_dev, meta_width // 2)),
            jnp.broadcast_to(own_target[:, None], (samples_dev, meta_width // 2)),
        ],
        axis=1,
    )
    rows = jnp.concatenate([own_embed, meta], axis=1)
    got = lax.all_to_all(
        jnp.broadcast_to(rows[None], (n_dp,) + rows.shape), "dp", 0, 0, tiled=True
    ).reshape(n_dp * samples_dev, rows.shape[1])
    all_embed = got[:, :emb_width]
    all_scale = got[:, emb_width]
    all_target = got[:, emb_width + meta_width // 2].astype(jnp.int32)
    losses, emb_grads = losses_and_grads(all_embed, all_scale, all_target)
    row_start = dp_index * samples_dev
    own_loss = lax.dynamic_slice_in_dim(losses, row_start, samples_dev, 0)
    own_grad = lax.dynamic_slice_in_dim(emb_grads, row_start, samples_dev, 0)
    return (own_loss[:, None], own_grad[:, None, :])


def solution(mesh):
    placed = (
        P("dp", "expert", None),
        P("dp", "expert"),
        P("expert", None, "dp"),
        P("expert", "dp", None),
        P(),
        P("dp", None),
        P(),
        P("dp", "expert"),
        P("dp", "expert"),
    )
    return jax.shard_map(
        shards,
        mesh=mesh,
        in_specs=placed,
        out_specs=(P("dp", "expert"), P("dp", "expert", None)),
        check_vma=False,
    )
```

```python
import jax
import jax.numpy as jnp
from jax import lax
from jax.sharding import PartitionSpec as P

PATCH = 64
EMPTY = 64.0


def group_losses(raw_rows, anchor_scale, target_index):
    member_count = raw_rows.shape[0]
    norm_square = jnp.sum(raw_rows * raw_rows, axis=-1, keepdims=True)
    unit_rows = raw_rows / jnp.sqrt(norm_square + 1e-06)
    scores = anchor_scale[:, None] * jnp.dot(
        unit_rows, unit_rows.T, precision=lax.Precision.HIGHEST
    )
    member = jnp.arange(member_count, dtype=jnp.int32)
    is_self = member[:, None] == member[None, :]
    denominator = jnp.sum(jnp.where(is_self, 0.0, jnp.exp(scores)), axis=-1)
    positive = jnp.sum(jnp.where(member[None, :] == target_index[:, None], scores, 0.0), axis=-1)
    return jnp.log(denominator) - positive


def losses_and_grads(raw_rows, anchor_scale, target_index):
    losses, pullback = jax.vjp(
        lambda rows_in: group_losses(rows_in, anchor_scale, target_index), raw_rows
    )
    (row_grads,) = pullback(jnp.ones_like(losses))
    return (losses, row_grads)


def ring_gather(piece, dp_index, n_dp, experts):
    flip = experts // 2
    size = n_dp * experts
    up = []
    for d in range(n_dp):
        for e in range(experts):
            to = (d + 1, e) if d + 1 < n_dp else (0, e ^ flip)
            up.append((d * experts + e, to[0] * experts + to[1]))
    down = [(b, a) for a, b in up]
    assert len(set(b for _, b in up)) == size
    rows = piece.shape[0]
    out = jnp.zeros((n_dp, rows) + piece.shape[1:], piece.dtype)
    out = lax.dynamic_update_index_in_dim(out, piece, dp_index, 0)
    from_below = piece
    from_above = piece
    reach = n_dp // 2
    for step in range(1, reach):
        from_below = lax.ppermute(from_below, ("dp", "expert"), up)
        from_above = lax.ppermute(from_above, ("dp", "expert"), down)
        out = lax.dynamic_update_index_in_dim(out, from_below, (dp_index - step) % n_dp, 0)
        out = lax.dynamic_update_index_in_dim(out, from_above, (dp_index + step) % n_dp, 0)
    last_below = lax.ppermute(from_below[: rows // 2], ("dp", "expert"), up)
    last_above = lax.ppermute(from_above[rows // 2 :], ("dp", "expert"), down)
    last = jnp.concatenate([last_below, last_above], axis=0)
    out = lax.dynamic_update_index_in_dim(out, last, (dp_index + reach) % n_dp, 0)
    return out.reshape((n_dp * rows,) + piece.shape[1:])


def ring_flood(arr, e_idx, experts, stride, ring):
    pos = (e_idx // stride) % ring

    def moved(e, step):
        digit = (e // stride) % ring
        return e + (((digit + step) % ring) - digit) * stride

    right = [(e, moved(e, 1)) for e in range(experts)]
    left = [(e, moved(e, -1)) for e in range(experts)]
    from_left = lax.ppermute(arr, "expert", right)
    from_right = lax.ppermute(arr, "expert", left)
    half = arr.shape[0] // 2
    far = jnp.concatenate(
        [
            lax.ppermute(from_left[:half], "expert", right),
            lax.ppermute(from_right[half:], "expert", left),
        ],
        axis=0,
    )
    out = jnp.zeros((ring,) + arr.shape, arr.dtype)
    out = lax.dynamic_update_index_in_dim(out, arr, pos, 0)
    out = lax.dynamic_update_index_in_dim(out, from_left, (pos - 1) % ring, 0)
    out = lax.dynamic_update_index_in_dim(out, from_right, (pos + 1) % ring, 0)
    out = lax.dynamic_update_index_in_dim(out, far, (pos + 2) % ring, 0)
    return out


def shards(
    tokens,
    assignment,
    up_weight,
    down_weight,
    mode_bias,
    projection,
    logit_scale,
    modality,
    pair_index,
):
    tok_rows = tokens.shape[0]
    model_width = tokens.shape[2]
    experts = lax.axis_size("expert")
    n_dp = lax.axis_size("dp")
    capacity = 2 * tok_rows // experts
    samples_dev = tok_rows // PATCH
    dp_index = lax.axis_index("dp")
    own_tokens = tokens[:, 0, :]
    own_assign = assignment[:, 0]
    expert_ids = jnp.arange(experts, dtype=jnp.int32)
    one_hot = (own_assign[:, None] == expert_ids[None, :]).astype(jnp.int32)
    running = jnp.cumsum(one_hot, axis=0)
    rank_in = jnp.sum(one_hot * (running - 1), axis=1)
    slot_ids = own_assign * capacity + rank_in
    n_slots = experts * capacity
    slot_of = (slot_ids[None, :] == jnp.arange(n_slots, dtype=jnp.int32)[:, None]).astype(
        jnp.bfloat16
    )
    send_rows = jnp.dot(slot_of, own_tokens, preferred_element_type=jnp.float32)
    is_empty = jnp.sum(slot_of.astype(jnp.float32), axis=1) < 0.5
    first_col = jnp.arange(model_width, dtype=jnp.int32) == 0
    send_rows = jnp.where(is_empty[:, None] & first_col[None, :], EMPTY, send_rows)
    send_rows = send_rows.astype(jnp.bfloat16).reshape(experts, capacity, model_width)
    recv_rows = lax.all_to_all(send_rows, "expert", split_axis=0, concat_axis=0, tiled=True)
    is_valid = recv_rows[:, :, 0] < EMPTY * 0.5
    src_totals = jnp.sum(is_valid.astype(jnp.int32), axis=1)
    offsets = jnp.cumsum(src_totals) - src_totals
    slot_pos = jnp.arange(capacity, dtype=jnp.int32)
    dest_rows = jnp.where(is_valid, offsets[:, None] + slot_pos[None, :], tok_rows)
    row_of = (
        dest_rows.reshape(1, -1) == jnp.arange(tok_rows, dtype=jnp.int32)[:, None]
    ).astype(jnp.bfloat16)
    compact = jnp.dot(
        row_of, recv_rows.reshape(-1, model_width), preferred_element_type=jnp.float32
    ).astype(jnp.bfloat16)
    up_local = up_weight[0]
    down_local = down_weight[0]
    e_idx = lax.axis_index("expert")
    ring = 4
    plane = 2 * ring * ring
    piece_rows = projection.shape[0] // plane
    piece = lax.dynamic_slice_in_dim(projection, (e_idx % plane) * piece_rows, piece_rows, 0)
    by_block = ring_gather(piece, dp_index, n_dp, experts).reshape(
        (n_dp, piece_rows) + projection.shape[1:]
    )
    core = e_idx % 2
    sibling = lax.ppermute(by_block, "expert", [(e, e ^ 1) for e in range(experts)])
    pair = jnp.where(
        core == 0, jnp.stack([by_block, sibling], axis=1), jnp.stack([sibling, by_block], axis=1)
    )
    along_x = ring_flood(pair, e_idx, experts, 2, ring)
    along_y = ring_flood(along_x.transpose(1, 0, 2, 3, 4), e_idx, experts, 2 * ring, ring)
    head = along_y.transpose(1, 0, 2, 3, 4, 5).reshape(
        projection.shape[0] * n_dp, projection.shape[1]
    )
    fold = jnp.dot(down_local, head, preferred_element_type=jnp.float32)
    fold_hi = fold.astype(jnp.bfloat16)
    fold_lo = (fold - fold_hi.astype(jnp.float32)).astype(jnp.bfloat16)
    token_sum = jnp.sum(
        own_tokens.reshape(samples_dev, PATCH, model_width), axis=1, dtype=jnp.float32
    )
    own_mode = modality[:, 0]
    mode_ids = jnp.arange(mode_bias.shape[0], dtype=jnp.int32)
    mode_match = own_mode[:, None] == mode_ids[None, :]
    bias_rows = jnp.sum(jnp.where(mode_match[:, :, None], mode_bias[None, :, :], 0.0), axis=1)
    base = token_sum / PATCH + bias_rows
    base_embed = jnp.dot(base, head.astype(jnp.float32), precision=lax.Precision.HIGHEST)
    base_embed, fold_hi, fold_lo = lax.optimization_barrier((base_embed, fold_hi, fold_lo))
    hidden = jax.nn.gelu(
        jnp.dot(
            lax.all_gather(compact, "dp", axis=0, tiled=True),
            up_local,
            preferred_element_type=jnp.float32,
        ),
        approximate=False,
    ).astype(jnp.bfloat16)
    part_embed = jnp.dot(hidden, fold_hi, preferred_element_type=jnp.float32) + jnp.dot(
        hidden, fold_lo, preferred_element_type=jnp.float32
    )
    expert_out = lax.psum_scatter(
        part_embed.astype(jnp.bfloat16), "dp", scatter_dimension=0, tiled=True
    )
    emb_width = expert_out.shape[1]
    slot_out = jnp.dot(row_of.T, expert_out, preferred_element_type=jnp.float32)
    returned = lax.all_to_all(
        slot_out.astype(jnp.bfloat16).reshape(experts, capacity, emb_width),
        "expert",
        split_axis=0,
        concat_axis=0,
        tiled=True,
    )
    sample_of = (
        jnp.arange(tok_rows, dtype=jnp.int32)[None, :] // PATCH
        == jnp.arange(samples_dev, dtype=jnp.int32)[:, None]
    ).astype(jnp.bfloat16)
    pool_of = jnp.dot(sample_of, slot_of.T, preferred_element_type=jnp.float32).astype(
        jnp.bfloat16
    )
    ffn_pool = jnp.dot(
        pool_of, returned.reshape(n_slots, emb_width), preferred_element_type=jnp.float32
    )
    own_embed = ffn_pool / PATCH + base_embed
    own_scale = jnp.sum(jnp.where(mode_match, logit_scale[None, :], 0.0), axis=1)
    own_target = pair_index[:, 0].astype(jnp.float32)
    meta_width = 128
    meta = jnp.concatenate(
        [
            jnp.broadcast_to(own_scale[:, None], (samples_dev, meta_width // 2)),
            jnp.broadcast_to(own_target[:, None], (samples_dev, meta_width // 2)),
        ],
        axis=1,
    )
    rows = jnp.concatenate([own_embed, meta], axis=1)
    got = lax.all_to_all(
        jnp.broadcast_to(rows[None], (n_dp,) + rows.shape), "dp", 0, 0, tiled=True
    ).reshape(n_dp * samples_dev, rows.shape[1])
    all_embed = got[:, :emb_width]
    all_scale = got[:, emb_width]
    all_target = got[:, emb_width + meta_width // 2].astype(jnp.int32)
    losses, emb_grads = losses_and_grads(all_embed, all_scale, all_target)
    row_start = dp_index * samples_dev
    own_loss = lax.dynamic_slice_in_dim(losses, row_start, samples_dev, 0)
    own_grad = lax.dynamic_slice_in_dim(emb_grads, row_start, samples_dev, 0)
    return (own_loss[:, None], own_grad[:, None, :])


def solution(mesh):
    placed = (
        P("dp", "expert", None),
        P("dp", "expert"),
        P("expert", None, "dp"),
        P("expert", "dp", None),
        P(),
        P("dp", None),
        P(),
        P("dp", "expert"),
        P("dp", "expert"),
    )
    return jax.shard_map(
        shards,
        mesh=mesh,
        in_specs=placed,
        out_specs=(P("dp", "expert"), P("dp", "expert", None)),
        check_vma=False,
    )
```

```python
import jax
import jax.numpy as jnp
from jax import lax
from jax.sharding import PartitionSpec as P

PATCH = 64
EMPTY = 64.0


def group_losses(raw_rows, anchor_scale, target_index):
    member_count = raw_rows.shape[0]
    norm_square = jnp.sum(raw_rows * raw_rows, axis=-1, keepdims=True)
    unit_rows = raw_rows / jnp.sqrt(norm_square + 1e-06)
    scores = anchor_scale[:, None] * jnp.dot(
        unit_rows, unit_rows.T, precision=lax.Precision.HIGHEST
    )
    member = jnp.arange(member_count, dtype=jnp.int32)
    is_self = member[:, None] == member[None, :]
    denominator = jnp.sum(jnp.where(is_self, 0.0, jnp.exp(scores)), axis=-1)
    positive = jnp.sum(jnp.where(member[None, :] == target_index[:, None], scores, 0.0), axis=-1)
    return jnp.log(denominator) - positive


def losses_and_grads(raw_rows, anchor_scale, target_index):
    losses, pullback = jax.vjp(
        lambda rows_in: group_losses(rows_in, anchor_scale, target_index), raw_rows
    )
    (row_grads,) = pullback(jnp.ones_like(losses))
    return (losses, row_grads)


def ring_gather(piece, dp_index, n_dp, experts):
    flip = experts // 2
    size = n_dp * experts
    up = []
    for d in range(n_dp):
        for e in range(experts):
            to = (d + 1, e) if d + 1 < n_dp else (0, e ^ flip)
            up.append((d * experts + e, to[0] * experts + to[1]))
    down = [(b, a) for a, b in up]
    assert len(set(b for _, b in up)) == size
    rows = piece.shape[0]
    out = jnp.zeros((n_dp, rows) + piece.shape[1:], piece.dtype)
    out = lax.dynamic_update_index_in_dim(out, piece, dp_index, 0)
    from_below = piece
    from_above = piece
    reach = n_dp // 2
    for step in range(1, reach):
        from_below = lax.ppermute(from_below, ("dp", "expert"), up)
        from_above = lax.ppermute(from_above, ("dp", "expert"), down)
        out = lax.dynamic_update_index_in_dim(out, from_below, (dp_index - step) % n_dp, 0)
        out = lax.dynamic_update_index_in_dim(out, from_above, (dp_index + step) % n_dp, 0)
    last_below = lax.ppermute(from_below[: rows // 2], ("dp", "expert"), up)
    last_above = lax.ppermute(from_above[rows // 2 :], ("dp", "expert"), down)
    last = jnp.concatenate([last_below, last_above], axis=0)
    out = lax.dynamic_update_index_in_dim(out, last, (dp_index + reach) % n_dp, 0)
    return out.reshape((n_dp * rows,) + piece.shape[1:])


def ring_flood(arr, e_idx, experts, stride, ring):
    pos = (e_idx // stride) % ring

    def moved(e, step):
        digit = (e // stride) % ring
        return e + (((digit + step) % ring) - digit) * stride

    right = [(e, moved(e, 1)) for e in range(experts)]
    left = [(e, moved(e, -1)) for e in range(experts)]
    from_left = lax.ppermute(arr, "expert", right)
    from_right = lax.ppermute(arr, "expert", left)
    half = arr.shape[0] // 2
    far = jnp.concatenate(
        [
            lax.ppermute(from_left[:half], "expert", right),
            lax.ppermute(from_right[half:], "expert", left),
        ],
        axis=0,
    )
    out = jnp.zeros((ring,) + arr.shape, arr.dtype)
    out = lax.dynamic_update_index_in_dim(out, arr, pos, 0)
    out = lax.dynamic_update_index_in_dim(out, from_left, (pos - 1) % ring, 0)
    out = lax.dynamic_update_index_in_dim(out, from_right, (pos + 1) % ring, 0)
    out = lax.dynamic_update_index_in_dim(out, far, (pos + 2) % ring, 0)
    return out


def shards(
    tokens,
    assignment,
    up_weight,
    down_weight,
    mode_bias,
    projection,
    logit_scale,
    modality,
    pair_index,
):
    tok_rows = tokens.shape[0]
    model_width = tokens.shape[2]
    experts = lax.axis_size("expert")
    n_dp = lax.axis_size("dp")
    capacity = 2 * tok_rows // experts
    samples_dev = tok_rows // PATCH
    dp_index = lax.axis_index("dp")
    own_tokens = tokens[:, 0, :]
    own_assign = assignment[:, 0]
    expert_ids = jnp.arange(experts, dtype=jnp.int32)
    one_hot = (own_assign[:, None] == expert_ids[None, :]).astype(jnp.int32)
    running = jnp.cumsum(one_hot, axis=0)
    rank_in = jnp.sum(one_hot * (running - 1), axis=1)
    slot_ids = own_assign * capacity + rank_in
    n_slots = experts * capacity
    slot_of = (slot_ids[None, :] == jnp.arange(n_slots, dtype=jnp.int32)[:, None]).astype(
        jnp.bfloat16
    )
    send_rows = jnp.dot(slot_of, own_tokens, preferred_element_type=jnp.float32)
    is_empty = jnp.sum(slot_of.astype(jnp.float32), axis=1) < 0.5
    first_col = jnp.arange(model_width, dtype=jnp.int32) == 0
    send_rows = jnp.where(is_empty[:, None] & first_col[None, :], EMPTY, send_rows)
    send_rows = send_rows.astype(jnp.bfloat16).reshape(experts, capacity, model_width)
    e_idx = lax.axis_index("expert")
    ring = 4
    plane = 2 * ring * ring
    piece_rows = projection.shape[0] // plane
    piece = lax.dynamic_slice_in_dim(projection, (e_idx % plane) * piece_rows, piece_rows, 0)
    by_block = ring_gather(piece, dp_index, n_dp, experts).reshape(
        (n_dp, piece_rows) + projection.shape[1:]
    )
    by_block, send_rows = lax.optimization_barrier((by_block, send_rows))
    recv_rows = lax.all_to_all(send_rows, "expert", split_axis=0, concat_axis=0, tiled=True)
    is_valid = recv_rows[:, :, 0] < EMPTY * 0.5
    src_totals = jnp.sum(is_valid.astype(jnp.int32), axis=1)
    offsets = jnp.cumsum(src_totals) - src_totals
    slot_pos = jnp.arange(capacity, dtype=jnp.int32)
    dest_rows = jnp.where(is_valid, offsets[:, None] + slot_pos[None, :], tok_rows)
    row_of = (
        dest_rows.reshape(1, -1) == jnp.arange(tok_rows, dtype=jnp.int32)[:, None]
    ).astype(jnp.bfloat16)
    compact = jnp.dot(
        row_of, recv_rows.reshape(-1, model_width), preferred_element_type=jnp.float32
    ).astype(jnp.bfloat16)
    up_local = up_weight[0]
    down_local = down_weight[0]
    core = e_idx % 2
    sibling = lax.ppermute(by_block, "expert", [(e, e ^ 1) for e in range(experts)])
    pair = jnp.where(
        core == 0, jnp.stack([by_block, sibling], axis=1), jnp.stack([sibling, by_block], axis=1)
    )
    along_x = ring_flood(pair, e_idx, experts, 2, ring)
    along_y = ring_flood(along_x.transpose(1, 0, 2, 3, 4), e_idx, experts, 2 * ring, ring)
    head = along_y.transpose(1, 0, 2, 3, 4, 5).reshape(
        projection.shape[0] * n_dp, projection.shape[1]
    )
    fold = jnp.dot(down_local, head, preferred_element_type=jnp.float32)
    fold_hi = fold.astype(jnp.bfloat16)
    fold_lo = (fold - fold_hi.astype(jnp.float32)).astype(jnp.bfloat16)
    token_sum = jnp.sum(
        own_tokens.reshape(samples_dev, PATCH, model_width), axis=1, dtype=jnp.float32
    )
    own_mode = modality[:, 0]
    mode_ids = jnp.arange(mode_bias.shape[0], dtype=jnp.int32)
    mode_match = own_mode[:, None] == mode_ids[None, :]
    bias_rows = jnp.sum(jnp.where(mode_match[:, :, None], mode_bias[None, :, :], 0.0), axis=1)
    base = token_sum / PATCH + bias_rows
    base_embed = jnp.dot(base, head.astype(jnp.float32), precision=lax.Precision.HIGHEST)
    base_embed, fold_hi, fold_lo = lax.optimization_barrier((base_embed, fold_hi, fold_lo))
    hidden = jax.nn.gelu(
        jnp.dot(
            lax.all_gather(compact, "dp", axis=0, tiled=True),
            up_local,
            preferred_element_type=jnp.float32,
        ),
        approximate=False,
    ).astype(jnp.bfloat16)
    part_embed = jnp.dot(hidden, fold_hi, preferred_element_type=jnp.float32) + jnp.dot(
        hidden, fold_lo, preferred_element_type=jnp.float32
    )
    expert_out = lax.psum_scatter(
        part_embed.astype(jnp.bfloat16), "dp", scatter_dimension=0, tiled=True
    )
    emb_width = expert_out.shape[1]
    slot_out = jnp.dot(row_of.T, expert_out, preferred_element_type=jnp.float32)
    returned = lax.all_to_all(
        slot_out.astype(jnp.bfloat16).reshape(experts, capacity, emb_width),
        "expert",
        split_axis=0,
        concat_axis=0,
        tiled=True,
    )
    sample_of = (
        jnp.arange(tok_rows, dtype=jnp.int32)[None, :] // PATCH
        == jnp.arange(samples_dev, dtype=jnp.int32)[:, None]
    ).astype(jnp.bfloat16)
    pool_of = jnp.dot(sample_of, slot_of.T, preferred_element_type=jnp.float32).astype(
        jnp.bfloat16
    )
    ffn_pool = jnp.dot(
        pool_of, returned.reshape(n_slots, emb_width), preferred_element_type=jnp.float32
    )
    own_embed = ffn_pool / PATCH + base_embed
    own_scale = jnp.sum(jnp.where(mode_match, logit_scale[None, :], 0.0), axis=1)
    own_target = pair_index[:, 0].astype(jnp.float32)
    meta_width = 128
    meta = jnp.concatenate(
        [
            jnp.broadcast_to(own_scale[:, None], (samples_dev, meta_width // 2)),
            jnp.broadcast_to(own_target[:, None], (samples_dev, meta_width // 2)),
        ],
        axis=1,
    )
    rows = jnp.concatenate([own_embed, meta], axis=1)
    got = lax.all_to_all(
        jnp.broadcast_to(rows[None], (n_dp,) + rows.shape), "dp", 0, 0, tiled=True
    ).reshape(n_dp * samples_dev, rows.shape[1])
    all_embed = got[:, :emb_width]
    all_scale = got[:, emb_width]
    all_target = got[:, emb_width + meta_width // 2].astype(jnp.int32)
    losses, emb_grads = losses_and_grads(all_embed, all_scale, all_target)
    row_start = dp_index * samples_dev
    own_loss = lax.dynamic_slice_in_dim(losses, row_start, samples_dev, 0)
    own_grad = lax.dynamic_slice_in_dim(emb_grads, row_start, samples_dev, 0)
    return (own_loss[:, None], own_grad[:, None, :])


def solution(mesh):
    placed = (
        P("dp", "expert", None),
        P("dp", "expert"),
        P("expert", None, "dp"),
        P("expert", "dp", None),
        P(),
        P("dp", None),
        P(),
        P("dp", "expert"),
        P("dp", "expert"),
    )
    return jax.shard_map(
        shards,
        mesh=mesh,
        in_specs=placed,
        out_specs=(P("dp", "expert"), P("dp", "expert", None)),
        check_vma=False,
    )
```

```python
import jax
import jax.numpy as jnp
from jax import lax
from jax.sharding import PartitionSpec as P

PATCH = 64
EMPTY = 64.0


def group_losses(raw_rows, anchor_scale, target_index):
    member_count = raw_rows.shape[0]
    norm_square = jnp.sum(raw_rows * raw_rows, axis=-1, keepdims=True)
    unit_rows = raw_rows / jnp.sqrt(norm_square + 1e-06)
    scores = anchor_scale[:, None] * jnp.dot(
        unit_rows, unit_rows.T, precision=lax.Precision.HIGHEST
    )
    member = jnp.arange(member_count, dtype=jnp.int32)
    is_self = member[:, None] == member[None, :]
    denominator = jnp.sum(jnp.where(is_self, 0.0, jnp.exp(scores)), axis=-1)
    positive = jnp.sum(jnp.where(member[None, :] == target_index[:, None], scores, 0.0), axis=-1)
    return jnp.log(denominator) - positive


def losses_and_grads(raw_rows, anchor_scale, target_index):
    losses, pullback = jax.vjp(
        lambda rows_in: group_losses(rows_in, anchor_scale, target_index), raw_rows
    )
    (row_grads,) = pullback(jnp.ones_like(losses))
    return (losses, row_grads)


def ring_gather(piece, dp_index, n_dp, experts):
    flip = experts // 2
    size = n_dp * experts
    up = []
    for d in range(n_dp):
        for e in range(experts):
            to = (d + 1, e) if d + 1 < n_dp else (0, e ^ flip)
            up.append((d * experts + e, to[0] * experts + to[1]))
    down = [(b, a) for a, b in up]
    assert len(set(b for _, b in up)) == size
    rows = piece.shape[0]
    out = jnp.zeros((n_dp, rows) + piece.shape[1:], piece.dtype)
    out = lax.dynamic_update_index_in_dim(out, piece, dp_index, 0)
    from_below = piece
    from_above = piece
    reach = n_dp // 2
    for step in range(1, reach):
        from_below = lax.ppermute(from_below, ("dp", "expert"), up)
        from_above = lax.ppermute(from_above, ("dp", "expert"), down)
        out = lax.dynamic_update_index_in_dim(out, from_below, (dp_index - step) % n_dp, 0)
        out = lax.dynamic_update_index_in_dim(out, from_above, (dp_index + step) % n_dp, 0)
    last_below = lax.ppermute(from_below[: rows // 2], ("dp", "expert"), up)
    last_above = lax.ppermute(from_above[rows // 2 :], ("dp", "expert"), down)
    last = jnp.concatenate([last_below, last_above], axis=0)
    out = lax.dynamic_update_index_in_dim(out, last, (dp_index + reach) % n_dp, 0)
    return out.reshape((n_dp * rows,) + piece.shape[1:])


def ring_flood(arr, e_idx, experts, stride, ring):
    pos = (e_idx // stride) % ring

    def moved(e, step):
        digit = (e // stride) % ring
        return e + (((digit + step) % ring) - digit) * stride

    right = [(e, moved(e, 1)) for e in range(experts)]
    left = [(e, moved(e, -1)) for e in range(experts)]
    from_left = lax.ppermute(arr, "expert", right)
    from_right = lax.ppermute(arr, "expert", left)
    half = arr.shape[0] // 2
    far = jnp.concatenate(
        [
            lax.ppermute(from_left[:half], "expert", right),
            lax.ppermute(from_right[half:], "expert", left),
        ],
        axis=0,
    )
    out = jnp.zeros((ring,) + arr.shape, arr.dtype)
    out = lax.dynamic_update_index_in_dim(out, arr, pos, 0)
    out = lax.dynamic_update_index_in_dim(out, from_left, (pos - 1) % ring, 0)
    out = lax.dynamic_update_index_in_dim(out, from_right, (pos + 1) % ring, 0)
    out = lax.dynamic_update_index_in_dim(out, far, (pos + 2) % ring, 0)
    return out


def shards(
    tokens,
    assignment,
    up_weight,
    down_weight,
    mode_bias,
    projection,
    logit_scale,
    modality,
    pair_index,
):
    tok_rows = tokens.shape[0]
    model_width = tokens.shape[2]
    experts = lax.axis_size("expert")
    n_dp = lax.axis_size("dp")
    capacity = 2 * tok_rows // experts
    samples_dev = tok_rows // PATCH
    dp_index = lax.axis_index("dp")
    own_tokens = tokens[:, 0, :]
    own_assign = assignment[:, 0]
    expert_ids = jnp.arange(experts, dtype=jnp.int32)
    one_hot = (own_assign[:, None] == expert_ids[None, :]).astype(jnp.int32)
    running = jnp.cumsum(one_hot, axis=0)
    rank_in = jnp.sum(one_hot * (running - 1), axis=1)
    slot_ids = own_assign * capacity + rank_in
    n_slots = experts * capacity
    slot_of = (slot_ids[None, :] == jnp.arange(n_slots, dtype=jnp.int32)[:, None]).astype(
        jnp.bfloat16
    )
    send_rows = jnp.einsum(
        "ejt,td->ejd",
        slot_of.reshape(experts, capacity, tok_rows),
        own_tokens,
        preferred_element_type=jnp.float32,
    )
    is_empty = jnp.sum(slot_of.astype(jnp.float32), axis=1).reshape(experts, capacity) < 0.5
    first_col = jnp.arange(model_width, dtype=jnp.int32) == 0
    send_rows = jnp.where(is_empty[:, :, None] & first_col[None, None, :], EMPTY, send_rows)
    send_rows = send_rows.astype(jnp.bfloat16)
    recv_rows = lax.all_to_all(send_rows, "expert", split_axis=0, concat_axis=0, tiled=True)
    is_valid = recv_rows[:, :, 0] < EMPTY * 0.5
    src_totals = jnp.sum(is_valid.astype(jnp.int32), axis=1)
    offsets = jnp.cumsum(src_totals) - src_totals
    slot_pos = jnp.arange(capacity, dtype=jnp.int32)
    dest_rows = jnp.where(is_valid, offsets[:, None] + slot_pos[None, :], tok_rows)
    row_of = (
        dest_rows.reshape(1, -1) == jnp.arange(tok_rows, dtype=jnp.int32)[:, None]
    ).astype(jnp.bfloat16)
    compact = jnp.einsum(
        "rej,ejd->rd",
        row_of.reshape(tok_rows, experts, capacity),
        recv_rows,
        preferred_element_type=jnp.float32,
    ).astype(jnp.bfloat16)
    up_local = up_weight[0]
    down_local = down_weight[0]
    e_idx = lax.axis_index("expert")
    ring = 4
    plane = 2 * ring * ring
    piece_rows = projection.shape[0] // plane
    piece = lax.dynamic_slice_in_dim(projection, (e_idx % plane) * piece_rows, piece_rows, 0)
    by_block = ring_gather(piece, dp_index, n_dp, experts).reshape(
        (n_dp, piece_rows) + projection.shape[1:]
    )
    core = e_idx % 2
    sibling = lax.ppermute(by_block, "expert", [(e, e ^ 1) for e in range(experts)])
    pair = jnp.where(
        core == 0, jnp.stack([by_block, sibling], axis=1), jnp.stack([sibling, by_block], axis=1)
    )
    along_x = ring_flood(pair, e_idx, experts, 2, ring)
    along_y = ring_flood(along_x.transpose(1, 0, 2, 3, 4), e_idx, experts, 2 * ring, ring)
    head = along_y.transpose(1, 0, 2, 3, 4, 5).reshape(
        projection.shape[0] * n_dp, projection.shape[1]
    )
    fold = jnp.dot(down_local, head, preferred_element_type=jnp.float32)
    fold_hi = fold.astype(jnp.bfloat16)
    fold_lo = (fold - fold_hi.astype(jnp.float32)).astype(jnp.bfloat16)
    token_sum = jnp.sum(
        own_tokens.reshape(samples_dev, PATCH, model_width), axis=1, dtype=jnp.float32
    )
    own_mode = modality[:, 0]
    mode_ids = jnp.arange(mode_bias.shape[0], dtype=jnp.int32)
    mode_match = own_mode[:, None] == mode_ids[None, :]
    bias_rows = jnp.sum(jnp.where(mode_match[:, :, None], mode_bias[None, :, :], 0.0), axis=1)
    base = token_sum / PATCH + bias_rows
    base_embed = jnp.dot(base, head.astype(jnp.float32), precision=lax.Precision.HIGHEST)
    base_embed, fold_hi, fold_lo = lax.optimization_barrier((base_embed, fold_hi, fold_lo))
    hidden = jax.nn.gelu(
        jnp.dot(
            lax.all_gather(compact, "dp", axis=0, tiled=True),
            up_local,
            preferred_element_type=jnp.float32,
        ),
        approximate=False,
    ).astype(jnp.bfloat16)
    part_embed = jnp.dot(hidden, fold_hi, preferred_element_type=jnp.float32) + jnp.dot(
        hidden, fold_lo, preferred_element_type=jnp.float32
    )
    expert_out = lax.psum_scatter(
        part_embed.astype(jnp.bfloat16), "dp", scatter_dimension=0, tiled=True
    )
    emb_width = expert_out.shape[1]
    slot_out = jnp.einsum(
        "rej,rd->ejd",
        row_of.reshape(tok_rows, experts, capacity),
        expert_out,
        preferred_element_type=jnp.float32,
    )
    returned = lax.all_to_all(
        slot_out.astype(jnp.bfloat16),
        "expert",
        split_axis=0,
        concat_axis=0,
        tiled=True,
    )
    sample_of = (
        jnp.arange(tok_rows, dtype=jnp.int32)[None, :] // PATCH
        == jnp.arange(samples_dev, dtype=jnp.int32)[:, None]
    ).astype(jnp.bfloat16)
    pool_of = jnp.dot(sample_of, slot_of.T, preferred_element_type=jnp.float32).astype(
        jnp.bfloat16
    )
    ffn_pool = jnp.einsum(
        "mej,ejd->md",
        pool_of.reshape(samples_dev, experts, capacity),
        returned,
        preferred_element_type=jnp.float32,
    )
    own_embed = ffn_pool / PATCH + base_embed
    own_scale = jnp.sum(jnp.where(mode_match, logit_scale[None, :], 0.0), axis=1)
    own_target = pair_index[:, 0].astype(jnp.float32)
    meta_width = 128
    meta = jnp.concatenate(
        [
            jnp.broadcast_to(own_scale[:, None], (samples_dev, meta_width // 2)),
            jnp.broadcast_to(own_target[:, None], (samples_dev, meta_width // 2)),
        ],
        axis=1,
    )
    rows = jnp.concatenate([own_embed, meta], axis=1)
    got = lax.all_to_all(
        jnp.broadcast_to(rows[None], (n_dp,) + rows.shape), "dp", 0, 0, tiled=True
    ).reshape(n_dp * samples_dev, rows.shape[1])
    all_embed = got[:, :emb_width]
    all_scale = got[:, emb_width]
    all_target = got[:, emb_width + meta_width // 2].astype(jnp.int32)
    losses, emb_grads = losses_and_grads(all_embed, all_scale, all_target)
    row_start = dp_index * samples_dev
    own_loss = lax.dynamic_slice_in_dim(losses, row_start, samples_dev, 0)
    own_grad = lax.dynamic_slice_in_dim(emb_grads, row_start, samples_dev, 0)
    return (own_loss[:, None], own_grad[:, None, :])


def solution(mesh):
    placed = (
        P("dp", "expert", None),
        P("dp", "expert"),
        P("expert", None, "dp"),
        P("expert", "dp", None),
        P(),
        P("dp", None),
        P(),
        P("dp", "expert"),
        P("dp", "expert"),
    )
    return jax.shard_map(
        shards,
        mesh=mesh,
        in_specs=placed,
        out_specs=(P("dp", "expert"), P("dp", "expert", None)),
        check_vma=False,
    )
```

```python
import jax
import jax.numpy as jnp
from jax import lax
from jax.sharding import PartitionSpec as P

PATCH = 64
EMPTY = 64.0


def group_losses(raw_rows, anchor_scale, target_index):
    member_count = raw_rows.shape[0]
    norm_square = jnp.sum(raw_rows * raw_rows, axis=-1, keepdims=True)
    unit_rows = raw_rows / jnp.sqrt(norm_square + 1e-06)
    scores = anchor_scale[:, None] * jnp.dot(
        unit_rows, unit_rows.T, precision=lax.Precision.HIGHEST
    )
    member = jnp.arange(member_count, dtype=jnp.int32)
    is_self = member[:, None] == member[None, :]
    denominator = jnp.sum(jnp.where(is_self, 0.0, jnp.exp(scores)), axis=-1)
    positive = jnp.sum(jnp.where(member[None, :] == target_index[:, None], scores, 0.0), axis=-1)
    return jnp.log(denominator) - positive


def losses_and_grads(raw_rows, anchor_scale, target_index):
    losses, pullback = jax.vjp(
        lambda rows_in: group_losses(rows_in, anchor_scale, target_index), raw_rows
    )
    (row_grads,) = pullback(jnp.ones_like(losses))
    return (losses, row_grads)


def ring_gather(piece, dp_index, n_dp, experts):
    flip = experts // 2
    size = n_dp * experts
    up = []
    for d in range(n_dp):
        for e in range(experts):
            to = (d + 1, e) if d + 1 < n_dp else (0, e ^ flip)
            up.append((d * experts + e, to[0] * experts + to[1]))
    down = [(b, a) for a, b in up]
    assert len(set(b for _, b in up)) == size
    rows = piece.shape[0]
    out = jnp.zeros((n_dp, rows) + piece.shape[1:], piece.dtype)
    out = lax.dynamic_update_index_in_dim(out, piece, dp_index, 0)
    from_below = piece
    from_above = piece
    reach = n_dp // 2
    for step in range(1, reach):
        from_below = lax.ppermute(from_below, ("dp", "expert"), up)
        from_above = lax.ppermute(from_above, ("dp", "expert"), down)
        out = lax.dynamic_update_index_in_dim(out, from_below, (dp_index - step) % n_dp, 0)
        out = lax.dynamic_update_index_in_dim(out, from_above, (dp_index + step) % n_dp, 0)
    last_below = lax.ppermute(from_below[: rows // 2], ("dp", "expert"), up)
    last_above = lax.ppermute(from_above[rows // 2 :], ("dp", "expert"), down)
    last = jnp.concatenate([last_below, last_above], axis=0)
    out = lax.dynamic_update_index_in_dim(out, last, (dp_index + reach) % n_dp, 0)
    return out.reshape((n_dp * rows,) + piece.shape[1:])


def ring_flood(arr, e_idx, experts, stride, ring):
    pos = (e_idx // stride) % ring

    def moved(e, step):
        digit = (e // stride) % ring
        return e + (((digit + step) % ring) - digit) * stride

    right = [(e, moved(e, 1)) for e in range(experts)]
    left = [(e, moved(e, -1)) for e in range(experts)]
    from_left = lax.ppermute(arr, "expert", right)
    from_right = lax.ppermute(arr, "expert", left)
    half = arr.shape[0] // 2
    far = jnp.concatenate(
        [
            lax.ppermute(from_left[:half], "expert", right),
            lax.ppermute(from_right[half:], "expert", left),
        ],
        axis=0,
    )
    out = jnp.zeros((ring,) + arr.shape, arr.dtype)
    out = lax.dynamic_update_index_in_dim(out, arr, pos, 0)
    out = lax.dynamic_update_index_in_dim(out, from_left, (pos - 1) % ring, 0)
    out = lax.dynamic_update_index_in_dim(out, from_right, (pos + 1) % ring, 0)
    out = lax.dynamic_update_index_in_dim(out, far, (pos + 2) % ring, 0)
    return out


def shards(
    tokens,
    assignment,
    up_weight,
    down_weight,
    mode_bias,
    projection,
    logit_scale,
    modality,
    pair_index,
):
    tok_rows = tokens.shape[0]
    model_width = tokens.shape[2]
    experts = lax.axis_size("expert")
    n_dp = lax.axis_size("dp")
    capacity = 2 * tok_rows // experts
    samples_dev = tok_rows // PATCH
    dp_index = lax.axis_index("dp")
    own_tokens = tokens[:, 0, :]
    own_assign = assignment[:, 0]
    expert_ids = jnp.arange(experts, dtype=jnp.int32)
    one_hot = (own_assign[:, None] == expert_ids[None, :]).astype(jnp.int32)
    running = jnp.cumsum(one_hot, axis=0)
    rank_in = jnp.sum(one_hot * (running - 1), axis=1)
    slot_ids = own_assign * capacity + rank_in
    n_slots = experts * capacity
    slot_of = (slot_ids[None, :] == jnp.arange(n_slots, dtype=jnp.int32)[:, None]).astype(
        jnp.bfloat16
    )
    send_rows = jnp.einsum(
        "ejt,td->ejd",
        slot_of.reshape(experts, capacity, tok_rows),
        own_tokens,
        preferred_element_type=jnp.float32,
    )
    is_empty = jnp.sum(slot_of.astype(jnp.float32), axis=1).reshape(experts, capacity) < 0.5
    first_col = jnp.arange(model_width, dtype=jnp.int32) == 0
    send_rows = jnp.where(is_empty[:, :, None] & first_col[None, None, :], EMPTY, send_rows)
    send_rows = send_rows.astype(jnp.bfloat16)
    recv_rows = lax.all_to_all(send_rows, "expert", split_axis=0, concat_axis=0, tiled=True)
    is_valid = recv_rows[:, :, 0] < EMPTY * 0.5
    src_totals = jnp.sum(is_valid.astype(jnp.int32), axis=1)
    offsets = jnp.cumsum(src_totals) - src_totals
    slot_pos = jnp.arange(capacity, dtype=jnp.int32)
    dest_rows = jnp.where(is_valid, offsets[:, None] + slot_pos[None, :], tok_rows)
    row_of = (
        dest_rows.reshape(1, -1) == jnp.arange(tok_rows, dtype=jnp.int32)[:, None]
    ).astype(jnp.bfloat16)
    compact = jnp.einsum(
        "rej,ejd->rd",
        row_of.reshape(tok_rows, experts, capacity),
        recv_rows,
        preferred_element_type=jnp.float32,
    ).astype(jnp.bfloat16)
    up_local = up_weight[0]
    down_local = down_weight[0]
    e_idx = lax.axis_index("expert")
    ring = 4
    plane = 2 * ring * ring
    piece_rows = projection.shape[0] // plane
    piece = lax.dynamic_slice_in_dim(projection, (e_idx % plane) * piece_rows, piece_rows, 0)
    by_block = lax.all_gather(piece, "dp", axis=0, tiled=True).reshape(
        (n_dp, piece_rows) + projection.shape[1:]
    )
    core = e_idx % 2
    sibling = lax.ppermute(by_block, "expert", [(e, e ^ 1) for e in range(experts)])
    pair = jnp.where(
        core == 0, jnp.stack([by_block, sibling], axis=1), jnp.stack([sibling, by_block], axis=1)
    )
    along_x = ring_flood(pair, e_idx, experts, 2, ring)
    along_y = ring_flood(along_x.transpose(1, 0, 2, 3, 4), e_idx, experts, 2 * ring, ring)
    head = along_y.transpose(1, 0, 2, 3, 4, 5).reshape(
        projection.shape[0] * n_dp, projection.shape[1]
    )
    fold = jnp.dot(down_local, head, preferred_element_type=jnp.float32)
    fold_hi = fold.astype(jnp.bfloat16)
    fold_lo = (fold - fold_hi.astype(jnp.float32)).astype(jnp.bfloat16)
    token_sum = jnp.sum(
        own_tokens.reshape(samples_dev, PATCH, model_width), axis=1, dtype=jnp.float32
    )
    own_mode = modality[:, 0]
    mode_ids = jnp.arange(mode_bias.shape[0], dtype=jnp.int32)
    mode_match = own_mode[:, None] == mode_ids[None, :]
    bias_rows = jnp.sum(jnp.where(mode_match[:, :, None], mode_bias[None, :, :], 0.0), axis=1)
    base = token_sum / PATCH + bias_rows
    base_embed = jnp.dot(base, head.astype(jnp.float32), precision=lax.Precision.HIGHEST)
    base_embed, fold_hi, fold_lo = lax.optimization_barrier((base_embed, fold_hi, fold_lo))
    hidden = jax.nn.gelu(
        jnp.dot(
            lax.all_gather(compact, "dp", axis=0, tiled=True),
            up_local,
            preferred_element_type=jnp.float32,
        ),
        approximate=False,
    ).astype(jnp.bfloat16)
    part_embed = jnp.dot(hidden, fold_hi, preferred_element_type=jnp.float32) + jnp.dot(
        hidden, fold_lo, preferred_element_type=jnp.float32
    )
    expert_out = lax.psum_scatter(
        part_embed.astype(jnp.bfloat16), "dp", scatter_dimension=0, tiled=True
    )
    emb_width = expert_out.shape[1]
    slot_out = jnp.einsum(
        "rej,rd->ejd",
        row_of.reshape(tok_rows, experts, capacity),
        expert_out,
        preferred_element_type=jnp.float32,
    )
    returned = lax.all_to_all(
        slot_out.astype(jnp.bfloat16),
        "expert",
        split_axis=0,
        concat_axis=0,
        tiled=True,
    )
    sample_of = (
        jnp.arange(tok_rows, dtype=jnp.int32)[None, :] // PATCH
        == jnp.arange(samples_dev, dtype=jnp.int32)[:, None]
    ).astype(jnp.bfloat16)
    pool_of = jnp.dot(sample_of, slot_of.T, preferred_element_type=jnp.float32).astype(
        jnp.bfloat16
    )
    ffn_pool = jnp.einsum(
        "mej,ejd->md",
        pool_of.reshape(samples_dev, experts, capacity),
        returned,
        preferred_element_type=jnp.float32,
    )
    own_embed = ffn_pool / PATCH + base_embed
    own_scale = jnp.sum(jnp.where(mode_match, logit_scale[None, :], 0.0), axis=1)
    own_target = pair_index[:, 0].astype(jnp.float32)
    meta_width = 128
    meta = jnp.concatenate(
        [
            jnp.broadcast_to(own_scale[:, None], (samples_dev, meta_width // 2)),
            jnp.broadcast_to(own_target[:, None], (samples_dev, meta_width // 2)),
        ],
        axis=1,
    )
    rows = jnp.concatenate([own_embed, meta], axis=1)
    got = lax.all_to_all(
        jnp.broadcast_to(rows[None], (n_dp,) + rows.shape), "dp", 0, 0, tiled=True
    ).reshape(n_dp * samples_dev, rows.shape[1])
    all_embed = got[:, :emb_width]
    all_scale = got[:, emb_width]
    all_target = got[:, emb_width + meta_width // 2].astype(jnp.int32)
    losses, emb_grads = losses_and_grads(all_embed, all_scale, all_target)
    row_start = dp_index * samples_dev
    own_loss = lax.dynamic_slice_in_dim(losses, row_start, samples_dev, 0)
    own_grad = lax.dynamic_slice_in_dim(emb_grads, row_start, samples_dev, 0)
    return (own_loss[:, None], own_grad[:, None, :])


def solution(mesh):
    placed = (
        P("dp", "expert", None),
        P("dp", "expert"),
        P("expert", None, "dp"),
        P("expert", "dp", None),
        P(),
        P("dp", None),
        P(),
        P("dp", "expert"),
        P("dp", "expert"),
    )
    return jax.shard_map(
        shards,
        mesh=mesh,
        in_specs=placed,
        out_specs=(P("dp", "expert"), P("dp", "expert", None)),
        check_vma=False,
    )
```

```python
import jax
import jax.numpy as jnp
from jax import lax
from jax.sharding import PartitionSpec as P

PATCH = 64
EMPTY = 64.0


def group_losses(raw_rows, anchor_scale, target_index):
    member_count = raw_rows.shape[0]
    norm_square = jnp.sum(raw_rows * raw_rows, axis=-1, keepdims=True)
    unit_rows = raw_rows / jnp.sqrt(norm_square + 1e-06)
    scores = anchor_scale[:, None] * jnp.dot(
        unit_rows, unit_rows.T, precision=lax.Precision.HIGHEST
    )
    member = jnp.arange(member_count, dtype=jnp.int32)
    is_self = member[:, None] == member[None, :]
    denominator = jnp.sum(jnp.where(is_self, 0.0, jnp.exp(scores)), axis=-1)
    positive = jnp.sum(jnp.where(member[None, :] == target_index[:, None], scores, 0.0), axis=-1)
    return jnp.log(denominator) - positive


def losses_and_grads(raw_rows, anchor_scale, target_index):
    losses, pullback = jax.vjp(
        lambda rows_in: group_losses(rows_in, anchor_scale, target_index), raw_rows
    )
    (row_grads,) = pullback(jnp.ones_like(losses))
    return (losses, row_grads)


def ring_gather(piece, dp_index, n_dp, experts):
    flip = experts // 2
    size = n_dp * experts
    up = []
    for d in range(n_dp):
        for e in range(experts):
            to = (d + 1, e) if d + 1 < n_dp else (0, e ^ flip)
            up.append((d * experts + e, to[0] * experts + to[1]))
    down = [(b, a) for a, b in up]
    assert len(set(b for _, b in up)) == size
    rows = piece.shape[0]
    out = jnp.zeros((n_dp, rows) + piece.shape[1:], piece.dtype)
    out = lax.dynamic_update_index_in_dim(out, piece, dp_index, 0)
    from_below = piece
    from_above = piece
    reach = n_dp // 2
    for step in range(1, reach):
        from_below = lax.ppermute(from_below, ("dp", "expert"), up)
        from_above = lax.ppermute(from_above, ("dp", "expert"), down)
        out = lax.dynamic_update_index_in_dim(out, from_below, (dp_index - step) % n_dp, 0)
        out = lax.dynamic_update_index_in_dim(out, from_above, (dp_index + step) % n_dp, 0)
    last_below = lax.ppermute(from_below[: rows // 2], ("dp", "expert"), up)
    last_above = lax.ppermute(from_above[rows // 2 :], ("dp", "expert"), down)
    last = jnp.concatenate([last_below, last_above], axis=0)
    out = lax.dynamic_update_index_in_dim(out, last, (dp_index + reach) % n_dp, 0)
    return out.reshape((n_dp * rows,) + piece.shape[1:])


def ring_flood(arr, e_idx, experts, stride, ring):
    pos = (e_idx // stride) % ring

    def moved(e, step):
        digit = (e // stride) % ring
        return e + (((digit + step) % ring) - digit) * stride

    right = [(e, moved(e, 1)) for e in range(experts)]
    left = [(e, moved(e, -1)) for e in range(experts)]
    from_left = lax.ppermute(arr, "expert", right)
    from_right = lax.ppermute(arr, "expert", left)
    half = arr.shape[0] // 2
    far = jnp.concatenate(
        [
            lax.ppermute(from_left[:half], "expert", right),
            lax.ppermute(from_right[half:], "expert", left),
        ],
        axis=0,
    )
    out = jnp.zeros((ring,) + arr.shape, arr.dtype)
    out = lax.dynamic_update_index_in_dim(out, arr, pos, 0)
    out = lax.dynamic_update_index_in_dim(out, from_left, (pos - 1) % ring, 0)
    out = lax.dynamic_update_index_in_dim(out, from_right, (pos + 1) % ring, 0)
    out = lax.dynamic_update_index_in_dim(out, far, (pos + 2) % ring, 0)
    return out


def shards(
    tokens,
    assignment,
    up_weight,
    down_weight,
    mode_bias,
    projection,
    logit_scale,
    modality,
    pair_index,
):
    tok_rows = tokens.shape[0]
    model_width = tokens.shape[2]
    experts = lax.axis_size("expert")
    n_dp = lax.axis_size("dp")
    capacity = 2 * tok_rows // experts
    samples_dev = tok_rows // PATCH
    dp_index = lax.axis_index("dp")
    own_tokens = tokens[:, 0, :]
    own_assign = assignment[:, 0]
    expert_ids = jnp.arange(experts, dtype=jnp.int32)
    one_hot = (own_assign[:, None] == expert_ids[None, :]).astype(jnp.int32)
    running = jnp.cumsum(one_hot, axis=0)
    rank_in = jnp.sum(one_hot * (running - 1), axis=1)
    slot_ids = own_assign * capacity + rank_in
    n_slots = experts * capacity
    slot_of = (slot_ids[None, :] == jnp.arange(n_slots, dtype=jnp.int32)[:, None]).astype(
        jnp.bfloat16
    )
    send_rows = jnp.einsum(
        "ejt,td->ejd",
        slot_of.reshape(experts, capacity, tok_rows),
        own_tokens,
        preferred_element_type=jnp.float32,
    )
    is_empty = jnp.sum(slot_of.astype(jnp.float32), axis=1).reshape(experts, capacity) < 0.5
    first_col = jnp.arange(model_width, dtype=jnp.int32) == 0
    send_rows = jnp.where(is_empty[:, :, None] & first_col[None, None, :], EMPTY, send_rows)
    send_rows = send_rows.astype(jnp.bfloat16)
    recv_rows = lax.all_to_all(send_rows, "expert", split_axis=0, concat_axis=0, tiled=True)
    is_valid = recv_rows[:, :, 0] < EMPTY * 0.5
    src_totals = jnp.sum(is_valid.astype(jnp.int32), axis=1)
    offsets = jnp.cumsum(src_totals) - src_totals
    slot_pos = jnp.arange(capacity, dtype=jnp.int32)
    dest_rows = jnp.where(is_valid, offsets[:, None] + slot_pos[None, :], tok_rows)
    row_of = (
        dest_rows.reshape(1, -1) == jnp.arange(tok_rows, dtype=jnp.int32)[:, None]
    ).astype(jnp.bfloat16)
    compact = jnp.einsum(
        "rej,ejd->rd",
        row_of.reshape(tok_rows, experts, capacity),
        recv_rows,
        preferred_element_type=jnp.float32,
    ).astype(jnp.bfloat16)
    up_local = up_weight[0]
    down_local = down_weight[0]
    e_idx = lax.axis_index("expert")
    ring = 4
    plane = 2 * ring * ring
    piece_rows = projection.shape[0] // plane
    piece = lax.dynamic_slice_in_dim(projection, (e_idx % plane) * piece_rows, piece_rows, 0)
    by_block = ring_gather(piece, dp_index, n_dp, experts).reshape(
        (n_dp, piece_rows) + projection.shape[1:]
    )
    core = e_idx % 2
    sibling = lax.ppermute(by_block, "expert", [(e, e ^ 1) for e in range(experts)])
    pair = jnp.where(
        core == 0, jnp.stack([by_block, sibling], axis=1), jnp.stack([sibling, by_block], axis=1)
    )
    along_x = ring_flood(pair, e_idx, experts, 2, ring)
    along_y = ring_flood(along_x.transpose(1, 0, 2, 3, 4), e_idx, experts, 2 * ring, ring)
    head = along_y.transpose(1, 0, 2, 3, 4, 5).reshape(
        projection.shape[0] * n_dp, projection.shape[1]
    )
    fold = jnp.dot(down_local, head, preferred_element_type=jnp.float32)
    fold_hi = fold.astype(jnp.bfloat16)
    token_sum = jnp.sum(
        own_tokens.reshape(samples_dev, PATCH, model_width), axis=1, dtype=jnp.float32
    )
    own_mode = modality[:, 0]
    mode_ids = jnp.arange(mode_bias.shape[0], dtype=jnp.int32)
    mode_match = own_mode[:, None] == mode_ids[None, :]
    bias_rows = jnp.sum(jnp.where(mode_match[:, :, None], mode_bias[None, :, :], 0.0), axis=1)
    base = token_sum / PATCH + bias_rows
    base_embed = jnp.dot(base, head.astype(jnp.float32), precision=lax.Precision.HIGHEST)
    base_embed, fold_hi = lax.optimization_barrier((base_embed, fold_hi))
    hidden = jax.nn.gelu(
        jnp.dot(
            lax.all_gather(compact, "dp", axis=0, tiled=True),
            up_local,
            preferred_element_type=jnp.float32,
        ),
        approximate=False,
    ).astype(jnp.bfloat16)
    part_embed = jnp.dot(hidden, fold_hi, preferred_element_type=jnp.float32)
    expert_out = lax.psum_scatter(
        part_embed.astype(jnp.bfloat16), "dp", scatter_dimension=0, tiled=True
    )
    emb_width = expert_out.shape[1]
    slot_out = jnp.einsum(
        "rej,rd->ejd",
        row_of.reshape(tok_rows, experts, capacity),
        expert_out,
        preferred_element_type=jnp.float32,
    )
    returned = lax.all_to_all(
        slot_out.astype(jnp.bfloat16),
        "expert",
        split_axis=0,
        concat_axis=0,
        tiled=True,
    )
    sample_of = (
        jnp.arange(tok_rows, dtype=jnp.int32)[None, :] // PATCH
        == jnp.arange(samples_dev, dtype=jnp.int32)[:, None]
    ).astype(jnp.bfloat16)
    pool_of = jnp.dot(sample_of, slot_of.T, preferred_element_type=jnp.float32).astype(
        jnp.bfloat16
    )
    ffn_pool = jnp.einsum(
        "mej,ejd->md",
        pool_of.reshape(samples_dev, experts, capacity),
        returned,
        preferred_element_type=jnp.float32,
    )
    own_embed = ffn_pool / PATCH + base_embed
    own_scale = jnp.sum(jnp.where(mode_match, logit_scale[None, :], 0.0), axis=1)
    own_target = pair_index[:, 0].astype(jnp.float32)
    meta_width = 128
    meta = jnp.concatenate(
        [
            jnp.broadcast_to(own_scale[:, None], (samples_dev, meta_width // 2)),
            jnp.broadcast_to(own_target[:, None], (samples_dev, meta_width // 2)),
        ],
        axis=1,
    )
    rows = jnp.concatenate([own_embed, meta], axis=1)
    got = lax.all_to_all(
        jnp.broadcast_to(rows[None], (n_dp,) + rows.shape), "dp", 0, 0, tiled=True
    ).reshape(n_dp * samples_dev, rows.shape[1])
    all_embed = got[:, :emb_width]
    all_scale = got[:, emb_width]
    all_target = got[:, emb_width + meta_width // 2].astype(jnp.int32)
    losses, emb_grads = losses_and_grads(all_embed, all_scale, all_target)
    row_start = dp_index * samples_dev
    own_loss = lax.dynamic_slice_in_dim(losses, row_start, samples_dev, 0)
    own_grad = lax.dynamic_slice_in_dim(emb_grads, row_start, samples_dev, 0)
    return (own_loss[:, None], own_grad[:, None, :])


def solution(mesh):
    placed = (
        P("dp", "expert", None),
        P("dp", "expert"),
        P("expert", None, "dp"),
        P("expert", "dp", None),
        P(),
        P("dp", None),
        P(),
        P("dp", "expert"),
        P("dp", "expert"),
    )
    return jax.shard_map(
        shards,
        mesh=mesh,
        in_specs=placed,
        out_specs=(P("dp", "expert"), P("dp", "expert", None)),
        check_vma=False,
    )
```

```python
import jax
import jax.numpy as jnp
from jax import lax
from jax.sharding import PartitionSpec as P

PATCH = 64
EMPTY = 64.0


def group_losses(raw_rows, anchor_scale, target_index):
    member_count = raw_rows.shape[0]
    norm_square = jnp.sum(raw_rows * raw_rows, axis=-1, keepdims=True)
    unit_rows = raw_rows / jnp.sqrt(norm_square + 1e-06)
    scores = anchor_scale[:, None] * jnp.dot(
        unit_rows, unit_rows.T, precision=lax.Precision.HIGHEST
    )
    member = jnp.arange(member_count, dtype=jnp.int32)
    is_self = member[:, None] == member[None, :]
    denominator = jnp.sum(jnp.where(is_self, 0.0, jnp.exp(scores)), axis=-1)
    positive = jnp.sum(jnp.where(member[None, :] == target_index[:, None], scores, 0.0), axis=-1)
    return jnp.log(denominator) - positive


def losses_and_grads(raw_rows, anchor_scale, target_index):
    losses, pullback = jax.vjp(
        lambda rows_in: group_losses(rows_in, anchor_scale, target_index), raw_rows
    )
    (row_grads,) = pullback(jnp.ones_like(losses))
    return (losses, row_grads)


def ring_gather(piece, dp_index, n_dp, experts):
    flip = experts // 2
    size = n_dp * experts
    up = []
    for d in range(n_dp):
        for e in range(experts):
            to = (d + 1, e) if d + 1 < n_dp else (0, e ^ flip)
            up.append((d * experts + e, to[0] * experts + to[1]))
    down = [(b, a) for a, b in up]
    assert len(set(b for _, b in up)) == size
    rows = piece.shape[0]
    out = jnp.zeros((n_dp, rows) + piece.shape[1:], piece.dtype)
    out = lax.dynamic_update_index_in_dim(out, piece, dp_index, 0)
    from_below = piece
    from_above = piece
    reach = n_dp // 2
    for step in range(1, reach):
        from_below = lax.ppermute(from_below, ("dp", "expert"), up)
        from_above = lax.ppermute(from_above, ("dp", "expert"), down)
        out = lax.dynamic_update_index_in_dim(out, from_below, (dp_index - step) % n_dp, 0)
        out = lax.dynamic_update_index_in_dim(out, from_above, (dp_index + step) % n_dp, 0)
    last_below = lax.ppermute(from_below[: rows // 2], ("dp", "expert"), up)
    last_above = lax.ppermute(from_above[rows // 2 :], ("dp", "expert"), down)
    last = jnp.concatenate([last_below, last_above], axis=0)
    out = lax.dynamic_update_index_in_dim(out, last, (dp_index + reach) % n_dp, 0)
    return out.reshape((n_dp * rows,) + piece.shape[1:])


def ring_flood(arr, e_idx, experts, stride, ring):
    pos = (e_idx // stride) % ring

    def moved(e, step):
        digit = (e // stride) % ring
        return e + (((digit + step) % ring) - digit) * stride

    right = [(e, moved(e, 1)) for e in range(experts)]
    left = [(e, moved(e, -1)) for e in range(experts)]
    from_left = lax.ppermute(arr, "expert", right)
    from_right = lax.ppermute(arr, "expert", left)
    half = arr.shape[0] // 2
    far = jnp.concatenate(
        [
            lax.ppermute(from_left[:half], "expert", right),
            lax.ppermute(from_right[half:], "expert", left),
        ],
        axis=0,
    )
    out = jnp.zeros((ring,) + arr.shape, arr.dtype)
    out = lax.dynamic_update_index_in_dim(out, arr, pos, 0)
    out = lax.dynamic_update_index_in_dim(out, from_left, (pos - 1) % ring, 0)
    out = lax.dynamic_update_index_in_dim(out, from_right, (pos + 1) % ring, 0)
    out = lax.dynamic_update_index_in_dim(out, far, (pos + 2) % ring, 0)
    return out


def shards(
    tokens,
    assignment,
    up_weight,
    down_weight,
    mode_bias,
    projection,
    logit_scale,
    modality,
    pair_index,
):
    tok_rows = tokens.shape[0]
    model_width = tokens.shape[2]
    experts = lax.axis_size("expert")
    n_dp = lax.axis_size("dp")
    capacity = 2 * tok_rows // experts
    samples_dev = tok_rows // PATCH
    dp_index = lax.axis_index("dp")
    own_tokens = tokens[:, 0, :]
    own_assign = assignment[:, 0]
    expert_ids = jnp.arange(experts, dtype=jnp.int32)
    one_hot = (own_assign[:, None] == expert_ids[None, :]).astype(jnp.int32)
    running = jnp.cumsum(one_hot, axis=0)
    rank_in = jnp.sum(one_hot * (running - 1), axis=1)
    slot_ids = own_assign * capacity + rank_in
    n_slots = experts * capacity
    slot_of = (slot_ids[None, :] == jnp.arange(n_slots, dtype=jnp.int32)[:, None]).astype(
        jnp.bfloat16
    )
    send_rows = jnp.einsum(
        "ejt,td->ejd",
        slot_of.reshape(experts, capacity, tok_rows),
        own_tokens,
        preferred_element_type=jnp.float32,
    )
    is_empty = jnp.sum(slot_of.astype(jnp.float32), axis=1).reshape(experts, capacity) < 0.5
    first_col = jnp.arange(model_width, dtype=jnp.int32) == 0
    send_rows = jnp.where(is_empty[:, :, None] & first_col[None, None, :], EMPTY, send_rows)
    send_rows = send_rows.astype(jnp.bfloat16)
    recv_rows = lax.all_to_all(send_rows, "expert", split_axis=0, concat_axis=0, tiled=True)
    is_valid = recv_rows[:, :, 0] < EMPTY * 0.5
    src_totals = jnp.sum(is_valid.astype(jnp.int32), axis=1)
    offsets = jnp.cumsum(src_totals) - src_totals
    slot_pos = jnp.arange(capacity, dtype=jnp.int32)
    dest_rows = jnp.where(is_valid, offsets[:, None] + slot_pos[None, :], tok_rows)
    row_of = (
        dest_rows.reshape(1, -1) == jnp.arange(tok_rows, dtype=jnp.int32)[:, None]
    ).astype(jnp.bfloat16)
    compact = jnp.einsum(
        "rej,ejd->rd",
        row_of.reshape(tok_rows, experts, capacity),
        recv_rows,
        preferred_element_type=jnp.float32,
    ).astype(jnp.bfloat16)
    up_local = up_weight[0]
    down_local = down_weight[0]
    e_idx = lax.axis_index("expert")
    ring = 4
    plane = 2 * ring * ring
    piece_rows = projection.shape[0] // plane
    piece = lax.dynamic_slice_in_dim(projection, (e_idx % plane) * piece_rows, piece_rows, 0)
    by_block = ring_gather(piece, dp_index, n_dp, experts).reshape(
        (n_dp, piece_rows) + projection.shape[1:]
    )
    core = e_idx % 2
    sibling = lax.ppermute(by_block, "expert", [(e, e ^ 1) for e in range(experts)])
    pair = jnp.where(
        core == 0, jnp.stack([by_block, sibling], axis=1), jnp.stack([sibling, by_block], axis=1)
    )
    along_x = ring_flood(pair, e_idx, experts, 2, ring)
    chunk_in = along_x.transpose(1, 0, 2, 3, 4)
    y_pos = (e_idx // (2 * ring)) % ring
    down_by_y = down_local.reshape(down_local.shape[0], n_dp, ring, -1)

    def fold_part(chunk, at):
        cols = lax.dynamic_index_in_dim(down_by_y, at, 2, keepdims=False)
        rows = chunk.reshape(n_dp, -1, projection.shape[1])
        return jnp.einsum("hbk,bkd->hd", cols, rows, preferred_element_type=jnp.float32)

    def y_moved(e, step):
        digit = (e // (2 * ring)) % ring
        return e + (((digit + step) % ring) - digit) * (2 * ring)

    y_right = [(e, y_moved(e, 1)) for e in range(experts)]
    y_left = [(e, y_moved(e, -1)) for e in range(experts)]
    fold = fold_part(chunk_in, y_pos)
    y_from_left = lax.ppermute(chunk_in, "expert", y_right)
    y_from_right = lax.ppermute(chunk_in, "expert", y_left)
    fold = fold + fold_part(y_from_left, (y_pos - 1) % ring)
    fold = fold + fold_part(y_from_right, (y_pos + 1) % ring)
    y_far = jnp.concatenate(
        [
            lax.ppermute(y_from_left[: n_dp // 2], "expert", y_right),
            lax.ppermute(y_from_right[n_dp // 2 :], "expert", y_left),
        ],
        axis=0,
    )
    fold = fold + fold_part(y_far, (y_pos + 2) % ring)
    head_parts = jnp.zeros((ring,) + chunk_in.shape, chunk_in.dtype)
    head_parts = lax.dynamic_update_index_in_dim(head_parts, chunk_in, y_pos, 0)
    head_parts = lax.dynamic_update_index_in_dim(head_parts, y_from_left, (y_pos - 1) % ring, 0)
    head_parts = lax.dynamic_update_index_in_dim(head_parts, y_from_right, (y_pos + 1) % ring, 0)
    head_parts = lax.dynamic_update_index_in_dim(head_parts, y_far, (y_pos + 2) % ring, 0)
    head = head_parts.transpose(1, 0, 2, 3, 4, 5).reshape(
        projection.shape[0] * n_dp, projection.shape[1]
    )
    fold_hi = fold.astype(jnp.bfloat16)
    fold_lo = (fold - fold_hi.astype(jnp.float32)).astype(jnp.bfloat16)
    token_sum = jnp.sum(
        own_tokens.reshape(samples_dev, PATCH, model_width), axis=1, dtype=jnp.float32
    )
    own_mode = modality[:, 0]
    mode_ids = jnp.arange(mode_bias.shape[0], dtype=jnp.int32)
    mode_match = own_mode[:, None] == mode_ids[None, :]
    bias_rows = jnp.sum(jnp.where(mode_match[:, :, None], mode_bias[None, :, :], 0.0), axis=1)
    base = token_sum / PATCH + bias_rows
    base_embed = jnp.dot(base, head.astype(jnp.float32), precision=lax.Precision.HIGHEST)
    base_embed, fold_hi, fold_lo = lax.optimization_barrier((base_embed, fold_hi, fold_lo))
    hidden = jax.nn.gelu(
        jnp.dot(
            lax.all_gather(compact, "dp", axis=0, tiled=True),
            up_local,
            preferred_element_type=jnp.float32,
        ),
        approximate=False,
    ).astype(jnp.bfloat16)
    part_embed = jnp.dot(hidden, fold_hi, preferred_element_type=jnp.float32) + jnp.dot(
        hidden, fold_lo, preferred_element_type=jnp.float32
    )
    expert_out = lax.psum_scatter(
        part_embed.astype(jnp.bfloat16), "dp", scatter_dimension=0, tiled=True
    )
    emb_width = expert_out.shape[1]
    slot_out = jnp.einsum(
        "rej,rd->ejd",
        row_of.reshape(tok_rows, experts, capacity),
        expert_out,
        preferred_element_type=jnp.float32,
    )
    returned = lax.all_to_all(
        slot_out.astype(jnp.bfloat16),
        "expert",
        split_axis=0,
        concat_axis=0,
        tiled=True,
    )
    sample_of = (
        jnp.arange(tok_rows, dtype=jnp.int32)[None, :] // PATCH
        == jnp.arange(samples_dev, dtype=jnp.int32)[:, None]
    ).astype(jnp.bfloat16)
    pool_of = jnp.dot(sample_of, slot_of.T, preferred_element_type=jnp.float32).astype(
        jnp.bfloat16
    )
    ffn_pool = jnp.einsum(
        "mej,ejd->md",
        pool_of.reshape(samples_dev, experts, capacity),
        returned,
        preferred_element_type=jnp.float32,
    )
    own_embed = ffn_pool / PATCH + base_embed
    own_scale = jnp.sum(jnp.where(mode_match, logit_scale[None, :], 0.0), axis=1)
    own_target = pair_index[:, 0].astype(jnp.float32)
    meta_width = 128
    meta = jnp.concatenate(
        [
            jnp.broadcast_to(own_scale[:, None], (samples_dev, meta_width // 2)),
            jnp.broadcast_to(own_target[:, None], (samples_dev, meta_width // 2)),
        ],
        axis=1,
    )
    rows = jnp.concatenate([own_embed, meta], axis=1)
    got = lax.all_to_all(
        jnp.broadcast_to(rows[None], (n_dp,) + rows.shape), "dp", 0, 0, tiled=True
    ).reshape(n_dp * samples_dev, rows.shape[1])
    all_embed = got[:, :emb_width]
    all_scale = got[:, emb_width]
    all_target = got[:, emb_width + meta_width // 2].astype(jnp.int32)
    losses, emb_grads = losses_and_grads(all_embed, all_scale, all_target)
    row_start = dp_index * samples_dev
    own_loss = lax.dynamic_slice_in_dim(losses, row_start, samples_dev, 0)
    own_grad = lax.dynamic_slice_in_dim(emb_grads, row_start, samples_dev, 0)
    return (own_loss[:, None], own_grad[:, None, :])


def solution(mesh):
    placed = (
        P("dp", "expert", None),
        P("dp", "expert"),
        P("expert", None, "dp"),
        P("expert", "dp", None),
        P(),
        P("dp", None),
        P(),
        P("dp", "expert"),
        P("dp", "expert"),
    )
    return jax.shard_map(
        shards,
        mesh=mesh,
        in_specs=placed,
        out_specs=(P("dp", "expert"), P("dp", "expert", None)),
        check_vma=False,
    )
```

```python
import jax
import jax.numpy as jnp
from jax import lax
from jax.sharding import PartitionSpec as P

PATCH = 64
EMPTY = 64.0


def group_losses(raw_rows, anchor_scale, target_index):
    member_count = raw_rows.shape[0]
    norm_square = jnp.sum(raw_rows * raw_rows, axis=-1, keepdims=True)
    unit_rows = raw_rows / jnp.sqrt(norm_square + 1e-06)
    scores = anchor_scale[:, None] * jnp.dot(
        unit_rows, unit_rows.T, precision=lax.Precision.HIGHEST
    )
    member = jnp.arange(member_count, dtype=jnp.int32)
    is_self = member[:, None] == member[None, :]
    denominator = jnp.sum(jnp.where(is_self, 0.0, jnp.exp(scores)), axis=-1)
    positive = jnp.sum(jnp.where(member[None, :] == target_index[:, None], scores, 0.0), axis=-1)
    return jnp.log(denominator) - positive


def losses_and_grads(raw_rows, anchor_scale, target_index):
    losses, pullback = jax.vjp(
        lambda rows_in: group_losses(rows_in, anchor_scale, target_index), raw_rows
    )
    (row_grads,) = pullback(jnp.ones_like(losses))
    return (losses, row_grads)


def ring_gather(piece, dp_index, n_dp, experts):
    flip = experts // 2
    size = n_dp * experts
    up = []
    for d in range(n_dp):
        for e in range(experts):
            to = (d + 1, e) if d + 1 < n_dp else (0, e ^ flip)
            up.append((d * experts + e, to[0] * experts + to[1]))
    down = [(b, a) for a, b in up]
    assert len(set(b for _, b in up)) == size
    rows = piece.shape[0]
    out = jnp.zeros((n_dp, rows) + piece.shape[1:], piece.dtype)
    out = lax.dynamic_update_index_in_dim(out, piece, dp_index, 0)
    from_below = piece
    from_above = piece
    reach = n_dp // 2
    for step in range(1, reach):
        from_below = lax.ppermute(from_below, ("dp", "expert"), up)
        from_above = lax.ppermute(from_above, ("dp", "expert"), down)
        out = lax.dynamic_update_index_in_dim(out, from_below, (dp_index - step) % n_dp, 0)
        out = lax.dynamic_update_index_in_dim(out, from_above, (dp_index + step) % n_dp, 0)
    last_below = lax.ppermute(from_below[: rows // 2], ("dp", "expert"), up)
    last_above = lax.ppermute(from_above[rows // 2 :], ("dp", "expert"), down)
    last = jnp.concatenate([last_below, last_above], axis=0)
    out = lax.dynamic_update_index_in_dim(out, last, (dp_index + reach) % n_dp, 0)
    return out.reshape((n_dp * rows,) + piece.shape[1:])


def ring_flood(arr, e_idx, experts, stride, ring):
    pos = (e_idx // stride) % ring

    def moved(e, step):
        digit = (e // stride) % ring
        return e + (((digit + step) % ring) - digit) * stride

    right = [(e, moved(e, 1)) for e in range(experts)]
    left = [(e, moved(e, -1)) for e in range(experts)]
    from_left = lax.ppermute(arr, "expert", right)
    from_right = lax.ppermute(arr, "expert", left)
    half = arr.shape[0] // 2
    far = jnp.concatenate(
        [
            lax.ppermute(from_left[:half], "expert", right),
            lax.ppermute(from_right[half:], "expert", left),
        ],
        axis=0,
    )
    out = jnp.zeros((ring,) + arr.shape, arr.dtype)
    out = lax.dynamic_update_index_in_dim(out, arr, pos, 0)
    out = lax.dynamic_update_index_in_dim(out, from_left, (pos - 1) % ring, 0)
    out = lax.dynamic_update_index_in_dim(out, from_right, (pos + 1) % ring, 0)
    out = lax.dynamic_update_index_in_dim(out, far, (pos + 2) % ring, 0)
    return out


def shards(
    tokens,
    assignment,
    up_weight,
    down_weight,
    mode_bias,
    projection,
    logit_scale,
    modality,
    pair_index,
):
    tok_rows = tokens.shape[0]
    model_width = tokens.shape[2]
    experts = lax.axis_size("expert")
    n_dp = lax.axis_size("dp")
    capacity = 2 * tok_rows // experts
    samples_dev = tok_rows // PATCH
    dp_index = lax.axis_index("dp")
    own_tokens = tokens[:, 0, :]
    own_assign = assignment[:, 0]
    expert_ids = jnp.arange(experts, dtype=jnp.int32)
    one_hot = (own_assign[:, None] == expert_ids[None, :]).astype(jnp.int32)
    running = jnp.cumsum(one_hot, axis=0)
    rank_in = jnp.sum(one_hot * (running - 1), axis=1)
    slot_ids = own_assign * capacity + rank_in
    n_slots = experts * capacity
    slot_of = (slot_ids[None, :] == jnp.arange(n_slots, dtype=jnp.int32)[:, None]).astype(
        jnp.bfloat16
    )
    send_rows = jnp.einsum(
        "ejt,td->ejd",
        slot_of.reshape(experts, capacity, tok_rows),
        own_tokens,
        preferred_element_type=jnp.float32,
    )
    is_empty = jnp.sum(slot_of.astype(jnp.float32), axis=1).reshape(experts, capacity) < 0.5
    first_col = jnp.arange(model_width, dtype=jnp.int32) == 0
    send_rows = jnp.where(is_empty[:, :, None] & first_col[None, None, :], EMPTY, send_rows)
    send_rows = send_rows.astype(jnp.bfloat16)
    recv_rows = lax.all_to_all(send_rows, "expert", split_axis=0, concat_axis=0, tiled=True)
    is_valid = recv_rows[:, :, 0] < EMPTY * 0.5
    src_totals = jnp.sum(is_valid.astype(jnp.int32), axis=1)
    before = (
        jnp.arange(experts, dtype=jnp.int32)[None, :] < jnp.arange(experts, dtype=jnp.int32)[:, None]
    ).astype(jnp.float32)
    offsets = jnp.dot(before, src_totals.astype(jnp.float32)).astype(jnp.int32)
    slot_pos = jnp.arange(capacity, dtype=jnp.int32)
    dest_rows = jnp.where(is_valid, offsets[:, None] + slot_pos[None, :], tok_rows)
    row_of = (
        dest_rows.reshape(1, -1) == jnp.arange(tok_rows, dtype=jnp.int32)[:, None]
    ).astype(jnp.bfloat16)
    compact = jnp.einsum(
        "rej,ejd->rd",
        row_of.reshape(tok_rows, experts, capacity),
        recv_rows,
        preferred_element_type=jnp.float32,
    ).astype(jnp.bfloat16)
    up_local = up_weight[0]
    down_local = down_weight[0]
    e_idx = lax.axis_index("expert")
    ring = 4
    plane = 2 * ring * ring
    piece_rows = projection.shape[0] // plane
    piece = lax.dynamic_slice_in_dim(projection, (e_idx % plane) * piece_rows, piece_rows, 0)
    by_block = ring_gather(piece, dp_index, n_dp, experts).reshape(
        (n_dp, piece_rows) + projection.shape[1:]
    )
    core = e_idx % 2
    sibling = lax.ppermute(by_block, "expert", [(e, e ^ 1) for e in range(experts)])
    pair = jnp.where(
        core == 0, jnp.stack([by_block, sibling], axis=1), jnp.stack([sibling, by_block], axis=1)
    )
    along_x = ring_flood(pair, e_idx, experts, 2, ring)
    along_y = ring_flood(along_x.transpose(1, 0, 2, 3, 4), e_idx, experts, 2 * ring, ring)
    head = along_y.transpose(1, 0, 2, 3, 4, 5).reshape(
        projection.shape[0] * n_dp, projection.shape[1]
    )
    fold = jnp.dot(down_local, head, preferred_element_type=jnp.float32)
    fold_hi = fold.astype(jnp.bfloat16)
    token_sum = jnp.sum(
        own_tokens.reshape(samples_dev, PATCH, model_width), axis=1, dtype=jnp.float32
    )
    own_mode = modality[:, 0]
    mode_ids = jnp.arange(mode_bias.shape[0], dtype=jnp.int32)
    mode_match = own_mode[:, None] == mode_ids[None, :]
    bias_rows = jnp.sum(jnp.where(mode_match[:, :, None], mode_bias[None, :, :], 0.0), axis=1)
    base = token_sum / PATCH + bias_rows
    base_embed = jnp.dot(base, head.astype(jnp.float32), precision=lax.Precision.HIGHEST)
    base_embed, fold_hi = lax.optimization_barrier((base_embed, fold_hi))
    hidden = jax.nn.gelu(
        jnp.dot(
            lax.all_gather(compact, "dp", axis=0, tiled=True),
            up_local,
            preferred_element_type=jnp.float32,
        ),
        approximate=False,
    ).astype(jnp.bfloat16)
    part_embed = jnp.dot(hidden, fold_hi, preferred_element_type=jnp.float32)
    expert_out = lax.psum_scatter(
        part_embed.astype(jnp.bfloat16), "dp", scatter_dimension=0, tiled=True
    )
    emb_width = expert_out.shape[1]
    slot_out = jnp.einsum(
        "rej,rd->ejd",
        row_of.reshape(tok_rows, experts, capacity),
        expert_out,
        preferred_element_type=jnp.float32,
    )
    returned = lax.all_to_all(
        slot_out.astype(jnp.bfloat16),
        "expert",
        split_axis=0,
        concat_axis=0,
        tiled=True,
    )
    sample_of = (
        jnp.arange(tok_rows, dtype=jnp.int32)[None, :] // PATCH
        == jnp.arange(samples_dev, dtype=jnp.int32)[:, None]
    ).astype(jnp.bfloat16)
    pool_of = jnp.dot(sample_of, slot_of.T, preferred_element_type=jnp.float32).astype(
        jnp.bfloat16
    )
    ffn_pool = jnp.einsum(
        "mej,ejd->md",
        pool_of.reshape(samples_dev, experts, capacity),
        returned,
        preferred_element_type=jnp.float32,
    )
    own_embed = ffn_pool / PATCH + base_embed
    own_scale = jnp.sum(jnp.where(mode_match, logit_scale[None, :], 0.0), axis=1)
    own_target = pair_index[:, 0].astype(jnp.float32)
    meta_width = 128
    meta = jnp.concatenate(
        [
            jnp.broadcast_to(own_scale[:, None], (samples_dev, meta_width // 2)),
            jnp.broadcast_to(own_target[:, None], (samples_dev, meta_width // 2)),
        ],
        axis=1,
    )
    rows = jnp.concatenate([own_embed, meta], axis=1)
    got = lax.all_to_all(
        jnp.broadcast_to(rows[None], (n_dp,) + rows.shape), "dp", 0, 0, tiled=True
    ).reshape(n_dp * samples_dev, rows.shape[1])
    all_embed = got[:, :emb_width]
    all_scale = got[:, emb_width]
    all_target = got[:, emb_width + meta_width // 2].astype(jnp.int32)
    losses, emb_grads = losses_and_grads(all_embed, all_scale, all_target)
    row_start = dp_index * samples_dev
    own_loss = lax.dynamic_slice_in_dim(losses, row_start, samples_dev, 0)
    own_grad = lax.dynamic_slice_in_dim(emb_grads, row_start, samples_dev, 0)
    return (own_loss[:, None], own_grad[:, None, :])


def solution(mesh):
    placed = (
        P("dp", "expert", None),
        P("dp", "expert"),
        P("expert", None, "dp"),
        P("expert", "dp", None),
        P(),
        P("dp", None),
        P(),
        P("dp", "expert"),
        P("dp", "expert"),
    )
    return jax.shard_map(
        shards,
        mesh=mesh,
        in_specs=placed,
        out_specs=(P("dp", "expert"), P("dp", "expert", None)),
        check_vma=False,
    )
```
